512 devices in a mesh: patch: 128 (over z, y, core), mp: 4 (over x).
Axes of the slice: x: 4, y: 4, z: 16, core: 2. Of those that a mesh axis runs over, the one named last changes fastest.
Arguments:
- features: bfloat16 [65536, 1024], P('patch'), may hold values from -16 to 16
- gain_attn: float32 [1024], replicated, may hold values from 0.1 to 1.9
- w_qkv: bfloat16 [3, 1024, 1024], P(None, None, 'mp'), as said below
- w_out: bfloat16 [1024, 1024], P('mp'), may hold values from -0.1875 to 0.1875
- gain_mlp: float32 [1024], replicated, may hold values from 0.1 to 1.9
- w_up: bfloat16 [1024, 2048], P(None, 'mp'), may hold values from -0.1875 to 0.1875
- w_down: bfloat16 [2048, 1024], P('mp'), may hold values from -0.125 to 0.125
- neighbours: int32 [512, 8], replicated, may hold values from 0 to 511, as said below
Outputs:
- layer_out: bfloat16 [65536, 1024], P('patch', 'mp')
The draws below stay inside these ranges and needn't reach their ends.
Inputs may be any that keep to these rules, and one draw needn't show every extreme that they name: `neighbours`: row p lists 8 different patches; the first is p itself. Patch q belongs to device q // 4 of the patch axis, and every listed patch belongs to a device whose index differs from that of p's device by at most 2 around the patch axis (the lining closes into a cycle). `w_qkv`: projection weights of mean zero.
All inputs are finite; a program needn't handle non-finite values.
Results may differ from the reference program's by a relative error of at most 0.012.
Values may be sent and summed in bfloat16 or wider, within the bound.
No kernel may reach another device: no remote copies, remote signals or barrier semaphores. Data moves between devices by JAX's collectives and lax.ppermute only.
A program may use at most 64 MiB of HBM per device.

```python
import jax
import jax.numpy as jnp
from jax import lax

D = 1024
H = 16
HD = 64
FF = 2048
PN = 128
K_NB = 8
REACH = 2
P_DEV = 4
NP = 512
NODES = 65536
N_MP = 4


def draw_neighbours(key, part):
    device_count = NP // P_DEV
    span = (2 * REACH + 1) * P_DEV
    patch_ids = jnp.arange(NP, dtype=jnp.int32)
    owner_dev = patch_ids // P_DEV
    candidate = jnp.arange(span, dtype=jnp.int32)
    cand_dev = jnp.mod(owner_dev[:, None] + candidate[None, :] // P_DEV - REACH, device_count)
    cand_ids = cand_dev * P_DEV + candidate[None, :] % P_DEV
    ranking = jax.random.randint(key, (NP, span), 0, 1 << 20, dtype=jnp.int32) * span + candidate[None, :]
    ranking = jnp.where(cand_ids == patch_ids[:, None], -1, ranking)
    ordering = jnp.argsort(ranking, axis=1)
    chosen = jnp.take_along_axis(cand_ids, ordering[:, :K_NB], axis=1)
    return chosen.astype(jnp.int32)


def draw_w_qkv(key, part):
    normal_base = jax.random.normal(key, (3, D, H * HD), jnp.float32) * D ** (-0.5)
    return normal_base.astype(jnp.bfloat16)


def draw_features(key, part):
    column_pos = jnp.arange(D, dtype=jnp.float32) / (D - 1.0)
    rough = jax.random.uniform(jax.random.fold_in(key, 3), (D,), jnp.float32, minval=0.7, maxval=1.3)
    col_scale = jnp.exp(jnp.log(0.35) + column_pos * (jnp.log(2.5) - jnp.log(0.35))) * rough
    base = jnp.clip(jax.random.normal(key, (NODES, D), jnp.float32), -5.0, 5.0)
    values = base * col_scale[None, :]
    return jnp.clip(values, -16.0, 16.0).astype(jnp.bfloat16)


def shard_levels(key, dims, cuts, low, top_value):
    loudness = 1.0
    for dim, shards_of in cuts:
        heights = jax.random.uniform(jax.random.fold_in(jax.random.fold_in(key, 6), dim), (shards_of,), jnp.float32, low / len(cuts), top_value / len(cuts))
        loudness = loudness * jnp.repeat(jnp.exp(heights), dims[dim] // shards_of).reshape((-1,) + (1,) * (len(dims) - 1 - dim))
    return loudness


def noise(own_key, dims, scale, most, split=(), held_as=jnp.bfloat16):
    level = shard_levels(own_key, dims, split, -0.22, 0.18) if split else 1.0
    array = jax.random.normal(own_key, dims, jnp.float32) * scale * level
    return jnp.minimum(jnp.maximum(array, -most), most).astype(held_as)


def setup_inputs(seed: int = 0) -> dict:
    streams_of = jax.random.split(jax.random.key(seed), 9)
    features = draw_features(jax.random.fold_in(streams_of[8], 71), 0)
    gain_attn = jnp.clip(1.0 + 0.18 * jax.random.normal(streams_of[1], (D,), jnp.float32), 0.1, 1.9)
    w_qkv = draw_w_qkv(jax.random.fold_in(streams_of[8], 71), 0)
    w_out = noise(streams_of[3], (H * HD, D), (H * HD) ** -0.5, 0.1875, ((0, 4),))
    gain_mlp = jnp.clip(1.0 + 0.18 * jax.random.normal(streams_of[4], (D,), jnp.float32), 0.1, 1.9)
    w_up = noise(streams_of[5], (D, FF), D ** -0.5, 0.1875, ((1, 4),))
    w_down = noise(streams_of[6], (FF, D), FF ** -0.5, 0.125, ((0, 4),))
    neighbours = draw_neighbours(jax.random.fold_in(streams_of[8], 71), 0)
    return dict(features=features, gain_attn=gain_attn, w_qkv=w_qkv, w_out=w_out, gain_mlp=gain_mlp, w_up=w_up, w_down=w_down, neighbours=neighbours)


def rms_norm(rows, gain):
    rows32 = rows.astype(jnp.float32)
    mean_sq = lax.optimization_barrier(jnp.mean(rows32 * rows32, axis=-1, keepdims=True))
    return (rows32 * lax.rsqrt(mean_sq + 1e-05) * gain).astype(jnp.bfloat16)

def group_sum(left, right, groups):
    width = left.shape[1] // groups
    total = jnp.zeros((left.shape[0], right.shape[1]), jnp.float32)
    for which in range(groups):
        term = jnp.dot(left[:, which * width:(which + 1) * width], right[which * width:(which + 1) * width], preferred_element_type=jnp.float32).astype(jnp.bfloat16)
        term = lax.optimization_barrier(term)
        total = total + term.astype(jnp.float32)
    return total

def reference(features, gain_attn, w_qkv, w_out, gain_mlp, w_up, w_down, neighbours):
    node_count = features.shape[0]
    normed = rms_norm(features, gain_attn)
    queries = jnp.dot(normed, w_qkv[0], preferred_element_type=jnp.float32).astype(jnp.bfloat16).reshape(NP, PN, H, HD)
    keys = jnp.dot(normed, w_qkv[1], preferred_element_type=jnp.float32).astype(jnp.bfloat16).reshape(NP, PN, H, HD)
    values = jnp.dot(normed, w_qkv[2], preferred_element_type=jnp.float32).astype(jnp.bfloat16).reshape(NP, PN, H, HD)
    scale_factor = 1.0 / HD ** 0.5

    def one_patch(inputs):
        query_blk, listed = inputs
        key_blk = keys[listed].reshape(K_NB * PN, H, HD)
        value_blk = values[listed].reshape(K_NB * PN, H, HD)
        scores = jnp.einsum('qhd,khd->hqk', query_blk.astype(jnp.float32), key_blk.astype(jnp.float32)) * scale_factor
        probs = jax.nn.softmax(scores, axis=-1).astype(jnp.bfloat16)
        mixed_rows = jnp.einsum('hqk,khd->qhd', probs.astype(jnp.float32), value_blk.astype(jnp.float32))
        return mixed_rows.astype(jnp.bfloat16).reshape(PN, H * HD)
    attended = lax.map(one_patch, (queries, neighbours)).reshape(node_count, H * HD)
    residual = features.astype(jnp.float32) + group_sum(attended, w_out, N_MP)
    normed2 = rms_norm(residual, gain_mlp)
    hidden = jax.nn.gelu(jnp.dot(normed2, w_up, preferred_element_type=jnp.float32), approximate=True).astype(jnp.bfloat16)
    return (residual + group_sum(hidden, w_down, N_MP)).astype(jnp.bfloat16)
```

```python
import jax
import jax.numpy as jnp
from jax import lax
from jax.sharding import PartitionSpec as P

D = 1024
HD = 64
PN = 128
K_NB = 8
REACH = 2


def from_behind(array, axis, by):
    length = lax.axis_size(axis)
    return lax.ppermute(array, axis, [(i, (i + by) % length) for i in range(length)])


def scatter_sum(parts, n_mp):
    rows, cols = parts.shape
    got = lax.all_to_all(parts.reshape(rows, n_mp, cols // n_mp), "mp", 1, 1)
    total = got[:, 0].astype(jnp.float32)
    for which in range(1, n_mp):
        total = total + got[:, which].astype(jnp.float32)
    return total


def gather_sum(vector, n_mp):
    got = lax.all_to_all(jnp.broadcast_to(vector[None], (n_mp,) + vector.shape), "mp", 0, 0)
    total = got[0]
    for which in range(1, n_mp):
        total = total + got[which]
    return total


def gather_cols(block, n_mp):
    rows, cols = block.shape
    spread = jnp.broadcast_to(block[:, None], (rows, n_mp, cols))
    return lax.all_to_all(spread, "mp", 1, 1).reshape(rows, n_mp * cols)


def normalize(rows, gain):
    rows32 = rows.astype(jnp.float32)
    mean_sq = jnp.mean(rows32 * rows32, axis=-1, keepdims=True)
    return (rows32 * lax.rsqrt(mean_sq + 1e-05) * gain).astype(jnp.bfloat16)


def per_device(features, gain_attn, w_qkv, w_out, gain_mlp, w_up, w_down, neighbours):
    row_count = features.shape[0]
    patches_here = row_count // PN
    heads_here = w_qkv.shape[2] // HD
    normed = normalize(features, gain_attn)
    queries = jnp.dot(normed, w_qkv[0], preferred_element_type=jnp.float32).astype(jnp.bfloat16)
    own_keys = (
        jnp.dot(normed, w_qkv[1], preferred_element_type=jnp.float32)
        .astype(jnp.bfloat16)
        .reshape(patches_here, PN, -1)
    )
    own_vals = (
        jnp.dot(normed, w_qkv[2], preferred_element_type=jnp.float32)
        .astype(jnp.bfloat16)
        .reshape(patches_here, PN, -1)
    )
    window = {0: (own_keys, own_vals)}
    for offset in range(-REACH, REACH + 1):
        if offset != 0:
            window[offset] = from_behind((own_keys, own_vals), "patch", -offset)
    keys_win = jnp.concatenate([window[offset][0] for offset in range(-REACH, REACH + 1)], axis=0)
    vals_win = jnp.concatenate([window[offset][1] for offset in range(-REACH, REACH + 1)], axis=0)
    device = lax.axis_index("patch")
    n_dev = lax.axis_size("patch")
    listed = lax.dynamic_slice_in_dim(neighbours, device * patches_here, patches_here, 0)
    owner_dev = listed // patches_here
    offset_dev = jnp.mod(owner_dev - device + n_dev // 2, n_dev) - n_dev // 2
    slot_index = (offset_dev + REACH) * patches_here + jnp.mod(listed, patches_here)
    keys_nb = keys_win[slot_index].reshape(patches_here, K_NB * PN, heads_here, HD)
    vals_nb = vals_win[slot_index].reshape(patches_here, K_NB * PN, heads_here, HD)
    query_blk = queries.reshape(patches_here, PN, heads_here, HD)
    scores = jnp.einsum(
        "pqhd,pkhd->phqk", query_blk, keys_nb, preferred_element_type=jnp.float32
    ) * (1.0 / HD**0.5)
    probs = jax.nn.softmax(scores, axis=-1).astype(jnp.bfloat16)
    mixed_rows = jnp.einsum("phqk,pkhd->pqhd", probs, vals_nb, preferred_element_type=jnp.float32)
    attended = mixed_rows.astype(jnp.bfloat16).reshape(row_count, heads_here * HD)
    n_mp = lax.axis_size("mp")
    partial_value = jnp.dot(attended, w_out, preferred_element_type=jnp.float32)
    col_share = scatter_sum(partial_value.astype(jnp.bfloat16), n_mp)
    col_width = col_share.shape[1]
    col_begin = lax.axis_index("mp") * col_width
    residual_cols = (
        lax.dynamic_slice_in_dim(features, col_begin, col_width, 1).astype(jnp.float32) + col_share
    )
    gain_cols = lax.dynamic_slice_in_dim(gain_mlp, col_begin, col_width, 0)
    square_sum = gather_sum(jnp.sum(residual_cols * residual_cols, axis=1), n_mp)
    inverse_rms = lax.rsqrt(square_sum / D + 1e-05)
    normed_cols = (residual_cols * inverse_rms[:, None] * gain_cols).astype(jnp.bfloat16)
    normed2 = gather_cols(normed_cols, n_mp)
    hidden = jax.nn.gelu(
        jnp.dot(normed2, w_up, preferred_element_type=jnp.float32), approximate=True
    ).astype(jnp.bfloat16)
    down_term = jnp.dot(hidden, w_down, preferred_element_type=jnp.float32)
    down_cols = scatter_sum(down_term.astype(jnp.bfloat16), n_mp)
    return (residual_cols + down_cols).astype(jnp.bfloat16)


def solution(mesh):
    return jax.shard_map(
        per_device,
        mesh=mesh,
        in_specs=(
            P("patch", None),
            P(),
            P(None, None, "mp"),
            P("mp", None),
            P(),
            P(None, "mp"),
            P("mp", None),
            P(),
        ),
        out_specs=P("patch", "mp"),
        check_vma=False,
    )
```

```python
import functools

import jax
import jax.numpy as jnp
from jax import lax
from jax.experimental import pallas as pl
from jax.sharding import PartitionSpec as P

D = 1024
HD = 64
PN = 128
K_NB = 8
REACH = 2


def from_behind(array, axis, by):
    length = lax.axis_size(axis)
    return lax.ppermute(array, axis, [(i, (i + by) % length) for i in range(length)])


def normalize(rows, gain):
    rows32 = rows.astype(jnp.float32)
    mean_sq = jnp.mean(rows32 * rows32, axis=-1, keepdims=True)
    return (rows32 * lax.rsqrt(mean_sq + 1e-05) * gain).astype(jnp.bfloat16)


def scatter_sum(parts, n_mp):
    rows, cols = parts.shape
    got = lax.all_to_all(parts.reshape(rows, n_mp, cols // n_mp), "mp", 1, 1)
    total = got[:, 0].astype(jnp.float32)
    for which in range(1, n_mp):
        total = total + got[:, which].astype(jnp.float32)
    return total


def gather_sum(vector, n_mp):
    got = lax.all_to_all(jnp.broadcast_to(vector[None], (n_mp,) + vector.shape), "mp", 0, 0)
    total = got[0]
    for which in range(1, n_mp):
        total = total + got[which]
    return total


def gather_cols(block, n_mp):
    rows, cols = block.shape
    spread = jnp.broadcast_to(block[:, None], (rows, n_mp, cols))
    return lax.all_to_all(spread, "mp", 1, 1).reshape(rows, n_mp * cols)


def window_attention(query_ref, bias_ref, *refs, n_heads, n_win):
    kv_refs, out_ref = refs[:n_win], refs[n_win]
    width = n_heads * HD
    win_rows = kv_refs[0].shape[0]
    bias = bias_ref[0]
    lane = lax.broadcasted_iota(jnp.int32, (PN, 2 * HD), 1)
    for pair in range(n_heads // 2):
        cols = slice(pair * 2 * HD, (pair + 1) * 2 * HD)
        q_pair = query_ref[:, cols]
        mixed = []
        for half in range(2):
            keep = (lane >= half * HD) & (lane < (half + 1) * HD)
            q_head = jnp.where(keep, q_pair, jnp.zeros_like(q_pair))
            scores = []
            for w in range(n_win):
                s = lax.dot_general(
                    q_head, kv_refs[w][:, cols], (((1,), (1,)), ((), ())),
                    preferred_element_type=jnp.float32,
                )
                scores.append(s * (1.0 / HD**0.5) + bias[:, w * win_rows:(w + 1) * win_rows])
            top = scores[0].max(axis=1, keepdims=True)
            for s in scores[1:]:
                top = jnp.maximum(top, s.max(axis=1, keepdims=True))
            exps = [jnp.exp(s - top) for s in scores]
            total = exps[0].sum(axis=1, keepdims=True)
            for e in exps[1:]:
                total = total + e.sum(axis=1, keepdims=True)
            acc = None
            for w in range(n_win):
                probs = (exps[w] / total).astype(jnp.bfloat16)
                v_cols = slice(width + pair * 2 * HD, width + (pair + 1) * 2 * HD)
                term = jnp.dot(probs, kv_refs[w][:, v_cols], preferred_element_type=jnp.float32)
                acc = term if acc is None else acc + term
            mixed.append(acc)
        out = jnp.where(lane < HD, mixed[0], mixed[1])
        out_ref[:, cols] = out.astype(out_ref.dtype)


def per_device(features, gain_attn, w_qkv, w_out, gain_mlp, w_up, w_down, neighbours):
    row_count = features.shape[0]
    patches_here = row_count // PN
    width = w_qkv.shape[2]
    heads_here = width // HD
    n_win = 2 * REACH + 1
    normed = normalize(features, gain_attn)
    w_all = jnp.concatenate([w_qkv[0], w_qkv[1], w_qkv[2]], axis=1)
    qkv = jnp.dot(normed, w_all, preferred_element_type=jnp.float32).astype(jnp.bfloat16)
    queries = qkv[:, :width]
    own_kv = qkv[:, width:]
    window = {0: own_kv}
    for offset in range(-REACH, REACH + 1):
        if offset != 0:
            window[offset] = from_behind(own_kv, "patch", -offset)
    device = lax.axis_index("patch")
    n_dev = lax.axis_size("patch")
    listed = lax.dynamic_slice_in_dim(neighbours, device * patches_here, patches_here, 0)
    owner_dev = listed // patches_here
    offset_dev = jnp.mod(owner_dev - device + n_dev // 2, n_dev) - n_dev // 2
    slot_index = (offset_dev + REACH) * patches_here + jnp.mod(listed, patches_here)
    slots = jnp.arange(n_win * patches_here, dtype=jnp.int32)
    chosen = jnp.any(slot_index[:, :, None] == slots[None, None, :], axis=1)
    bias = jnp.where(chosen, 0.0, -jnp.inf).astype(jnp.float32)
    bias = jnp.repeat(bias, PN, axis=1).reshape(patches_here, 1, n_win * patches_here * PN)
    kv_list = [window[offset] for offset in range(-REACH, REACH + 1)]
    kv_spec = pl.BlockSpec((row_count, 2 * width), lambda p: (0, 0))
    attended = pl.pallas_call(
        functools.partial(window_attention, n_heads=heads_here, n_win=n_win),
        grid=(patches_here,),
        in_specs=[
            pl.BlockSpec((PN, width), lambda p: (p, 0)),
            pl.BlockSpec((1, 1, n_win * row_count), lambda p: (p, 0, 0)),
        ]
        + [kv_spec] * n_win,
        out_specs=pl.BlockSpec((PN, width), lambda p: (p, 0)),
        out_shape=jax.ShapeDtypeStruct((row_count, width), jnp.bfloat16),
    )(queries, bias, *kv_list)
    n_mp = lax.axis_size("mp")
    partial_value = jnp.dot(attended, w_out, preferred_element_type=jnp.float32)
    col_share = scatter_sum(partial_value.astype(jnp.bfloat16), n_mp)
    col_width = col_share.shape[1]
    col_begin = lax.axis_index("mp") * col_width
    residual_cols = (
        lax.dynamic_slice_in_dim(features, col_begin, col_width, 1).astype(jnp.float32) + col_share
    )
    gain_cols = lax.dynamic_slice_in_dim(gain_mlp, col_begin, col_width, 0)
    square_sum = gather_sum(jnp.sum(residual_cols * residual_cols, axis=1), n_mp)
    inverse_rms = lax.rsqrt(square_sum / D + 1e-05)
    normed_cols = (residual_cols * inverse_rms[:, None] * gain_cols).astype(jnp.bfloat16)
    normed2 = gather_cols(normed_cols, n_mp)
    hidden = jax.nn.gelu(
        jnp.dot(normed2, w_up, preferred_element_type=jnp.float32), approximate=True
    ).astype(jnp.bfloat16)
    down_term = jnp.dot(hidden, w_down, preferred_element_type=jnp.float32)
    down_cols = scatter_sum(down_term.astype(jnp.bfloat16), n_mp)
    return (residual_cols + down_cols).astype(jnp.bfloat16)


def solution(mesh):
    return jax.shard_map(
        per_device,
        mesh=mesh,
        in_specs=(
            P("patch", None),
            P(),
            P(None, None, "mp"),
            P("mp", None),
            P(),
            P(None, "mp"),
            P("mp", None),
            P(),
        ),
        out_specs=P("patch", "mp"),
        check_vma=False,
    )
```

```python
import functools

import jax
import jax.numpy as jnp
from jax import lax
from jax.experimental import pallas as pl
from jax.sharding import PartitionSpec as P

D = 1024
HD = 64
PN = 128
K_NB = 8
REACH = 2


def from_behind(array, axis, by):
    length = lax.axis_size(axis)
    return lax.ppermute(array, axis, [(i, (i + by) % length) for i in range(length)])


def normalize(rows, gain):
    rows32 = rows.astype(jnp.float32)
    mean_sq = jnp.mean(rows32 * rows32, axis=-1, keepdims=True)
    return (rows32 * lax.rsqrt(mean_sq + 1e-05) * gain).astype(jnp.bfloat16)


def scatter_sum(parts, n_mp):
    rows, cols = parts.shape
    got = lax.all_to_all(parts.reshape(rows, n_mp, cols // n_mp), "mp", 1, 1)
    total = got[:, 0].astype(jnp.float32)
    for which in range(1, n_mp):
        total = total + got[:, which].astype(jnp.float32)
    return total


def gather_with_sums(block, vector, n_mp):
    rows, cols = block.shape
    pieces = []
    rest = vector
    for _ in range(3):
        piece = rest.astype(jnp.bfloat16)
        rest = rest - piece.astype(jnp.float32)
        pieces.append(piece.reshape(-1, cols))
    extra = jnp.concatenate(pieces, axis=0)
    pad = (-extra.shape[0]) % 8
    extra = jnp.concatenate([extra, jnp.zeros((pad, cols), jnp.bfloat16)], axis=0)
    packed = jnp.concatenate([block, extra], axis=0)
    spread = jnp.broadcast_to(packed[:, None], (packed.shape[0], n_mp, cols))
    got = lax.all_to_all(spread, "mp", 1, 1)
    gathered = got[:rows].reshape(rows, n_mp * cols)
    per_row = rows // cols
    sums = []
    for which in range(n_mp):
        bits = got[rows:rows + 3 * per_row, which].astype(jnp.float32).reshape(3, rows)
        sums.append((bits[0] + bits[1]) + bits[2])
    return gathered, sums


def window_attention(query_ref, bias_ref, *refs, n_heads, n_win):
    kv_refs, out_ref = refs[:n_win], refs[n_win]
    width = n_heads * HD
    win_rows = kv_refs[0].shape[0]
    bias = bias_ref[0]
    lane = lax.broadcasted_iota(jnp.int32, (PN, 2 * HD), 1)
    for pair in range(n_heads // 2):
        cols = slice(pair * 2 * HD, (pair + 1) * 2 * HD)
        q_pair = query_ref[:, cols]
        mixed = []
        for half in range(2):
            keep = (lane >= half * HD) & (lane < (half + 1) * HD)
            q_head = jnp.where(keep, q_pair, jnp.zeros_like(q_pair))
            scores = []
            for w in range(n_win):
                s = lax.dot_general(
                    q_head, kv_refs[w][:, cols], (((1,), (1,)), ((), ())),
                    preferred_element_type=jnp.float32,
                )
                scores.append(s * (1.0 / HD**0.5) + bias[:, w * win_rows:(w + 1) * win_rows])
            top = scores[0].max(axis=1, keepdims=True)
            for s in scores[1:]:
                top = jnp.maximum(top, s.max(axis=1, keepdims=True))
            exps = [jnp.exp(s - top) for s in scores]
            total = exps[0].sum(axis=1, keepdims=True)
            for e in exps[1:]:
                total = total + e.sum(axis=1, keepdims=True)
            acc = None
            for w in range(n_win):
                probs = (exps[w] / total).astype(jnp.bfloat16)
                v_cols = slice(width + pair * 2 * HD, width + (pair + 1) * 2 * HD)
                term = jnp.dot(probs, kv_refs[w][:, v_cols], preferred_element_type=jnp.float32)
                acc = term if acc is None else acc + term
            mixed.append(acc)
        out = jnp.where(lane < HD, mixed[0], mixed[1])
        out_ref[:, cols] = out.astype(out_ref.dtype)


def per_device(features, gain_attn, w_qkv, w_out, gain_mlp, w_up, w_down, neighbours):
    row_count = features.shape[0]
    patches_here = row_count // PN
    width = w_qkv.shape[2]
    heads_here = width // HD
    n_win = 2 * REACH + 1
    normed = normalize(features, gain_attn)
    w_all = jnp.concatenate([w_qkv[0], w_qkv[1], w_qkv[2]], axis=1)
    qkv = jnp.dot(normed, w_all, preferred_element_type=jnp.float32).astype(jnp.bfloat16)
    queries = qkv[:, :width]
    own_kv = qkv[:, width:]
    window = {0: own_kv}
    for offset in range(-REACH, REACH + 1):
        if offset != 0:
            window[offset] = from_behind(own_kv, "patch", -offset)
    device = lax.axis_index("patch")
    n_dev = lax.axis_size("patch")
    listed = lax.dynamic_slice_in_dim(neighbours, device * patches_here, patches_here, 0)
    owner_dev = listed // patches_here
    offset_dev = jnp.mod(owner_dev - device + n_dev // 2, n_dev) - n_dev // 2
    slot_index = (offset_dev + REACH) * patches_here + jnp.mod(listed, patches_here)
    slots = jnp.arange(n_win * patches_here, dtype=jnp.int32)
    chosen = jnp.any(slot_index[:, :, None] == slots[None, None, :], axis=1)
    bias = jnp.where(chosen, 0.0, -jnp.inf).astype(jnp.float32)
    bias = jnp.repeat(bias, PN, axis=1).reshape(patches_here, 1, n_win * patches_here * PN)
    kv_list = [window[offset] for offset in range(-REACH, REACH + 1)]
    kv_spec = pl.BlockSpec((row_count, 2 * width), lambda p: (0, 0))
    attended = pl.pallas_call(
        functools.partial(window_attention, n_heads=heads_here, n_win=n_win),
        grid=(patches_here,),
        in_specs=[
            pl.BlockSpec((PN, width), lambda p: (p, 0)),
            pl.BlockSpec((1, 1, n_win * row_count), lambda p: (p, 0, 0)),
        ]
        + [kv_spec] * n_win,
        out_specs=pl.BlockSpec((PN, width), lambda p: (p, 0)),
        out_shape=jax.ShapeDtypeStruct((row_count, width), jnp.bfloat16),
    )(queries, bias, *kv_list)
    n_mp = lax.axis_size("mp")
    partial_value = jnp.dot(attended, w_out, preferred_element_type=jnp.float32)
    col_share = scatter_sum(partial_value.astype(jnp.bfloat16), n_mp)
    col_width = col_share.shape[1]
    col_begin = lax.axis_index("mp") * col_width
    residual_cols = (
        lax.dynamic_slice_in_dim(features, col_begin, col_width, 1).astype(jnp.float32) + col_share
    )
    gain_cols = lax.dynamic_slice_in_dim(gain_mlp, col_begin, col_width, 0)
    scaled_cols = (residual_cols * gain_cols).astype(jnp.bfloat16)
    square_part = jnp.sum(residual_cols * residual_cols, axis=1)
    scaled, square_parts = gather_with_sums(scaled_cols, square_part, n_mp)
    square_sum = square_parts[0]
    for which in range(1, n_mp):
        square_sum = square_sum + square_parts[which]
    inverse_rms = lax.rsqrt(square_sum / D + 1e-05)
    normed2 = (scaled.astype(jnp.float32) * inverse_rms[:, None]).astype(jnp.bfloat16)
    hidden = jax.nn.gelu(
        jnp.dot(normed2, w_up, preferred_element_type=jnp.float32), approximate=True
    ).astype(jnp.bfloat16)
    down_term = jnp.dot(hidden, w_down, preferred_element_type=jnp.float32)
    down_cols = scatter_sum(down_term.astype(jnp.bfloat16), n_mp)
    return (residual_cols + down_cols).astype(jnp.bfloat16)


def solution(mesh):
    return jax.shard_map(
        per_device,
        mesh=mesh,
        in_specs=(
            P("patch", None),
            P(),
            P(None, None, "mp"),
            P("mp", None),
            P(),
            P(None, "mp"),
            P("mp", None),
            P(),
        ),
        out_specs=P("patch", "mp"),
        check_vma=False,
    )
```

```python
import functools

import jax
import jax.numpy as jnp
from jax import lax
from jax.experimental import pallas as pl
from jax.sharding import PartitionSpec as P

D = 1024
HD = 64
PN = 128
K_NB = 8
REACH = 2


def from_behind(array, axis, by):
    length = lax.axis_size(axis)
    return lax.ppermute(array, axis, [(i, (i + by) % length) for i in range(length)])


def normalize(rows, gain):
    rows32 = rows.astype(jnp.float32)
    mean_sq = jnp.mean(rows32 * rows32, axis=-1, keepdims=True)
    return (rows32 * lax.rsqrt(mean_sq + 1e-05) * gain).astype(jnp.bfloat16)


def scatter_sum(parts, n_mp):
    rows, cols = parts.shape
    got = lax.all_to_all(parts.reshape(rows, n_mp, cols // n_mp), "mp", 1, 1)
    total = got[:, 0].astype(jnp.float32)
    for which in range(1, n_mp):
        total = total + got[:, which].astype(jnp.float32)
    return total


def gather_cols(block, n_mp):
    rows, cols = block.shape
    spread = jnp.broadcast_to(block[:, None], (rows, n_mp, cols))
    return lax.all_to_all(spread, "mp", 1, 1).reshape(rows, n_mp * cols)


def window_attention(query_ref, bias_ref, *refs, n_heads, n_win):
    kv_refs, out_ref = refs[:n_win], refs[n_win]
    width = n_heads * HD
    win_rows = kv_refs[0].shape[0]
    bias = bias_ref[0]
    lane = lax.broadcasted_iota(jnp.int32, (PN, 2 * HD), 1)
    for pair in range(n_heads // 2):
        cols = slice(pair * 2 * HD, (pair + 1) * 2 * HD)
        q_pair = query_ref[:, cols]
        mixed = []
        for half in range(2):
            keep = (lane >= half * HD) & (lane < (half + 1) * HD)
            q_head = jnp.where(keep, q_pair, jnp.zeros_like(q_pair))
            scores = []
            for w in range(n_win):
                s = lax.dot_general(
                    q_head, kv_refs[w][:, cols], (((1,), (1,)), ((), ())),
                    preferred_element_type=jnp.float32,
                )
                scores.append(s * (1.0 / HD**0.5) + bias[:, w * win_rows:(w + 1) * win_rows])
            top = scores[0].max(axis=1, keepdims=True)
            for s in scores[1:]:
                top = jnp.maximum(top, s.max(axis=1, keepdims=True))
            exps = [jnp.exp(s - top) for s in scores]
            total = exps[0].sum(axis=1, keepdims=True)
            for e in exps[1:]:
                total = total + e.sum(axis=1, keepdims=True)
            acc = None
            for w in range(n_win):
                probs = (exps[w] / total).astype(jnp.bfloat16)
                v_cols = slice(width + pair * 2 * HD, width + (pair + 1) * 2 * HD)
                term = jnp.dot(probs, kv_refs[w][:, v_cols], preferred_element_type=jnp.float32)
                acc = term if acc is None else acc + term
            mixed.append(acc)
        out = jnp.where(lane < HD, mixed[0], mixed[1])
        out_ref[:, cols] = out.astype(out_ref.dtype)


def per_device(features, gain_attn, w_qkv, w_out, gain_mlp, w_up, w_down, neighbours):
    row_count = features.shape[0]
    patches_here = row_count // PN
    width = w_qkv.shape[2]
    heads_here = width // HD
    n_win = 2 * REACH + 1
    normed = normalize(features, gain_attn)
    w_all = jnp.concatenate([w_qkv[0], w_qkv[1], w_qkv[2]], axis=1)
    qkv = jnp.dot(normed, w_all, preferred_element_type=jnp.float32).astype(jnp.bfloat16)
    queries = qkv[:, :width]
    own_kv = qkv[:, width:]
    window = {0: own_kv}
    for offset in range(-REACH, REACH + 1):
        if offset != 0:
            window[offset] = from_behind(own_kv, "patch", -offset)
    device = lax.axis_index("patch")
    n_dev = lax.axis_size("patch")
    listed = lax.dynamic_slice_in_dim(neighbours, device * patches_here, patches_here, 0)
    owner_dev = listed // patches_here
    offset_dev = jnp.mod(owner_dev - device + n_dev // 2, n_dev) - n_dev // 2
    slot_index = (offset_dev + REACH) * patches_here + jnp.mod(listed, patches_here)
    slots = jnp.arange(n_win * patches_here, dtype=jnp.int32)
    chosen = jnp.any(slot_index[:, :, None] == slots[None, None, :], axis=1)
    bias = jnp.where(chosen, 0.0, -jnp.inf).astype(jnp.float32)
    bias = jnp.repeat(bias, PN, axis=1).reshape(patches_here, 1, n_win * patches_here * PN)
    kv_list = [window[offset] for offset in range(-REACH, REACH + 1)]
    kv_spec = pl.BlockSpec((row_count, 2 * width), lambda p: (0, 0))
    attended = pl.pallas_call(
        functools.partial(window_attention, n_heads=heads_here, n_win=n_win),
        grid=(patches_here,),
        in_specs=[
            pl.BlockSpec((PN, width), lambda p: (p, 0)),
            pl.BlockSpec((1, 1, n_win * row_count), lambda p: (p, 0, 0)),
        ]
        + [kv_spec] * n_win,
        out_specs=pl.BlockSpec((PN, width), lambda p: (p, 0)),
        out_shape=jax.ShapeDtypeStruct((row_count, width), jnp.bfloat16),
    )(queries, bias, *kv_list)
    n_mp = lax.axis_size("mp")
    partial_value = jnp.dot(attended, w_out, preferred_element_type=jnp.float32)
    col_share = scatter_sum(partial_value.astype(jnp.bfloat16), n_mp)
    col_width = col_share.shape[1]
    col_begin = lax.axis_index("mp") * col_width
    residual_cols = (
        lax.dynamic_slice_in_dim(features, col_begin, col_width, 1).astype(jnp.float32) + col_share
    )
    rows_full = gather_cols(residual_cols.astype(jnp.bfloat16), n_mp).astype(jnp.float32)
    square_sum = jnp.sum(rows_full * rows_full, axis=1, keepdims=True)
    inverse_rms = lax.rsqrt(square_sum / D + 1e-05)
    normed2 = (rows_full * inverse_rms * gain_mlp).astype(jnp.bfloat16)
    hidden = jax.nn.gelu(
        jnp.dot(normed2, w_up, preferred_element_type=jnp.float32), approximate=True
    ).astype(jnp.bfloat16)
    down_term = jnp.dot(hidden, w_down, preferred_element_type=jnp.float32)
    down_cols = scatter_sum(down_term.astype(jnp.bfloat16), n_mp)
    return (residual_cols + down_cols).astype(jnp.bfloat16)


def solution(mesh):
    return jax.shard_map(
        per_device,
        mesh=mesh,
        in_specs=(
            P("patch", None),
            P(),
            P(None, None, "mp"),
            P("mp", None),
            P(),
            P(None, "mp"),
            P("mp", None),
            P(),
        ),
        out_specs=P("patch", "mp"),
        check_vma=False,
    )
```

```python
import functools

import jax
import jax.numpy as jnp
from jax import lax
from jax.experimental import pallas as pl
from jax.experimental.pallas import tpu as pltpu
from jax.sharding import PartitionSpec as P

D = 1024
HD = 64
PN = 128
K_NB = 8
REACH = 2


def from_behind(array, axis, by):
    length = lax.axis_size(axis)
    return lax.ppermute(array, axis, [(i, (i + by) % length) for i in range(length)])


def normalize(rows, gain):
    rows32 = rows.astype(jnp.float32)
    mean_sq = jnp.mean(rows32 * rows32, axis=-1, keepdims=True)
    return (rows32 * lax.rsqrt(mean_sq + 1e-05) * gain).astype(jnp.bfloat16)


def scatter_sum(parts, n_mp):
    rows, cols = parts.shape
    got = lax.all_to_all(parts.reshape(rows, n_mp, cols // n_mp), "mp", 1, 1)
    total = got[:, 0].astype(jnp.float32)
    for which in range(1, n_mp):
        total = total + got[:, which].astype(jnp.float32)
    return total


def gather_sum(vector, n_mp):
    got = lax.all_to_all(jnp.broadcast_to(vector[None], (n_mp,) + vector.shape), "mp", 0, 0)
    total = got[0]
    for which in range(1, n_mp):
        total = total + got[which]
    return total


def gather_cols(block, n_mp):
    rows, cols = block.shape
    spread = jnp.broadcast_to(block[:, None], (rows, n_mp, cols))
    return lax.all_to_all(spread, "mp", 1, 1).reshape(rows, n_mp * cols)


def window_attention(slot_ref, query_ref, *refs, n_heads, n_win, n_nb):
    kv_refs, out_ref, gathered = refs[:n_win], refs[n_win], refs[n_win + 1]
    width = n_heads * HD
    per_win = kv_refs[0].shape[0] // PN
    patch = pl.program_id(0)
    for k in range(n_nb):
        slot = slot_ref[patch, k]
        block = slot // per_win
        local = slot % per_win
        for w in range(n_win):
            @pl.when(block == w)
            def _():
                gathered[k * PN:(k + 1) * PN, :] = kv_refs[w][pl.ds(pl.multiple_of(local * PN, PN), PN), :]
    lane = lax.broadcasted_iota(jnp.int32, (PN, 2 * HD), 1)
    for pair in range(n_heads // 2):
        cols = slice(pair * 2 * HD, (pair + 1) * 2 * HD)
        v_cols = slice(width + pair * 2 * HD, width + (pair + 1) * 2 * HD)
        q_pair = query_ref[:, cols]
        keys = gathered[:, cols]
        vals = gathered[:, v_cols]
        mixed = []
        for half in range(2):
            keep = (lane >= half * HD) & (lane < (half + 1) * HD)
            q_head = jnp.where(keep, q_pair, jnp.zeros_like(q_pair))
            s = lax.dot_general(
                q_head, keys, (((1,), (1,)), ((), ())), preferred_element_type=jnp.float32
            ) * (1.0 / HD**0.5)
            e = jnp.exp(s - s.max(axis=1, keepdims=True))
            inv = 1.0 / e.sum(axis=1, keepdims=True)
            probs = (e * inv).astype(jnp.bfloat16)
            mixed.append(jnp.dot(probs, vals, preferred_element_type=jnp.float32))
        out = jnp.where(lane < HD, mixed[0], mixed[1])
        out_ref[:, cols] = out.astype(out_ref.dtype)


def per_device(features, gain_attn, w_qkv, w_out, gain_mlp, w_up, w_down, neighbours):
    row_count = features.shape[0]
    patches_here = row_count // PN
    width = w_qkv.shape[2]
    heads_here = width // HD
    n_win = 2 * REACH + 1
    normed = normalize(features, gain_attn)
    w_all = jnp.concatenate([w_qkv[0], w_qkv[1], w_qkv[2]], axis=1)
    qkv = jnp.dot(normed, w_all, preferred_element_type=jnp.float32).astype(jnp.bfloat16)
    queries = qkv[:, :width]
    own_kv = qkv[:, width:]
    window = {0: own_kv}
    for offset in range(-REACH, REACH + 1):
        if offset != 0:
            window[offset] = from_behind(own_kv, "patch", -offset)
    device = lax.axis_index("patch")
    n_dev = lax.axis_size("patch")
    listed = lax.dynamic_slice_in_dim(neighbours, device * patches_here, patches_here, 0)
    owner_dev = listed // patches_here
    offset_dev = jnp.mod(owner_dev - device + n_dev // 2, n_dev) - n_dev // 2
    slot_index = (offset_dev + REACH) * patches_here + jnp.mod(listed, patches_here)
    kv_list = [window[offset] for offset in range(-REACH, REACH + 1)]
    kv_spec = pl.BlockSpec((row_count, 2 * width), lambda p, slots: (0, 0))
    attended = pl.pallas_call(
        functools.partial(window_attention, n_heads=heads_here, n_win=n_win, n_nb=K_NB),
        grid_spec=pltpu.PrefetchScalarGridSpec(
            num_scalar_prefetch=1,
            grid=(patches_here,),
            in_specs=[pl.BlockSpec((PN, width), lambda p, slots: (p, 0))] + [kv_spec] * n_win,
            out_specs=pl.BlockSpec((PN, width), lambda p, slots: (p, 0)),
            scratch_shapes=[pltpu.VMEM((K_NB * PN, 2 * width), jnp.bfloat16)],
        ),
        out_shape=jax.ShapeDtypeStruct((row_count, width), jnp.bfloat16),
    )(slot_index.astype(jnp.int32), queries, *kv_list)
    n_mp = lax.axis_size("mp")
    partial_value = jnp.dot(attended, w_out, preferred_element_type=jnp.float32)
    col_share = scatter_sum(partial_value.astype(jnp.bfloat16), n_mp)
    col_width = col_share.shape[1]
    col_begin = lax.axis_index("mp") * col_width
    residual_cols = (
        lax.dynamic_slice_in_dim(features, col_begin, col_width, 1).astype(jnp.float32) + col_share
    )
    gain_cols = lax.dynamic_slice_in_dim(gain_mlp, col_begin, col_width, 0)
    square_sum = gather_sum(jnp.sum(residual_cols * residual_cols, axis=1), n_mp)
    inverse_rms = lax.rsqrt(square_sum / D + 1e-05)
    normed_cols = (residual_cols * inverse_rms[:, None] * gain_cols).astype(jnp.bfloat16)
    normed2 = gather_cols(normed_cols, n_mp)
    hidden = jax.nn.gelu(
        jnp.dot(normed2, w_up, preferred_element_type=jnp.float32), approximate=True
    ).astype(jnp.bfloat16)
    down_term = jnp.dot(hidden, w_down, preferred_element_type=jnp.float32)
    down_cols = scatter_sum(down_term.astype(jnp.bfloat16), n_mp)
    return (residual_cols + down_cols).astype(jnp.bfloat16)


def solution(mesh):
    return jax.shard_map(
        per_device,
        mesh=mesh,
        in_specs=(
            P("patch", None),
            P(),
            P(None, None, "mp"),
            P("mp", None),
            P(),
            P(None, "mp"),
            P("mp", None),
            P(),
        ),
        out_specs=P("patch", "mp"),
        check_vma=False,
    )
```

```python
import functools

import jax
import jax.numpy as jnp
from jax import lax
from jax.experimental import pallas as pl
from jax.experimental.pallas import tpu as pltpu
from jax.sharding import PartitionSpec as P

D = 1024
HD = 64
PN = 128
K_NB = 8
REACH = 2
N_CHUNK = 2


def from_behind(array, axis, by):
    length = lax.axis_size(axis)
    return lax.ppermute(array, axis, [(i, (i + by) % length) for i in range(length)])


def normalize(rows, gain):
    rows32 = rows.astype(jnp.float32)
    mean_sq = jnp.mean(rows32 * rows32, axis=-1, keepdims=True)
    return (rows32 * lax.rsqrt(mean_sq + 1e-05) * gain).astype(jnp.bfloat16)


def scatter_sum(parts, n_mp):
    rows, cols = parts.shape
    got = lax.all_to_all(parts.reshape(rows, n_mp, cols // n_mp), "mp", 1, 1)
    total = got[:, 0].astype(jnp.float32)
    for which in range(1, n_mp):
        total = total + got[:, which].astype(jnp.float32)
    return total


def gather_sum(vector, n_mp):
    got = lax.all_to_all(jnp.broadcast_to(vector[None], (n_mp,) + vector.shape), "mp", 0, 0)
    total = got[0]
    for which in range(1, n_mp):
        total = total + got[which]
    return total


def gather_cols(block, n_mp):
    rows, cols = block.shape
    spread = jnp.broadcast_to(block[:, None], (rows, n_mp, cols))
    return lax.all_to_all(spread, "mp", 1, 1).reshape(rows, n_mp * cols)


def window_attention(slot_ref, query_ref, *refs, n_heads, n_win, n_nb):
    kv_refs, out_ref, gathered = refs[:n_win], refs[n_win], refs[n_win + 1]
    width = n_heads * HD
    per_win = kv_refs[0].shape[0] // PN
    patch = pl.program_id(0)
    for k in range(n_nb):
        slot = slot_ref[patch, k]
        block = slot // per_win
        local = slot % per_win
        for w in range(n_win):
            @pl.when(block == w)
            def _():
                gathered[k * PN:(k + 1) * PN, :] = kv_refs[w][pl.ds(pl.multiple_of(local * PN, PN), PN), :]
    lane = lax.broadcasted_iota(jnp.int32, (PN, 2 * HD), 1)
    for pair in range(n_heads // 2):
        cols = slice(pair * 2 * HD, (pair + 1) * 2 * HD)
        v_cols = slice(width + pair * 2 * HD, width + (pair + 1) * 2 * HD)
        q_pair = query_ref[:, cols]
        keys = gathered[:, cols]
        vals = gathered[:, v_cols]
        mixed = []
        for half in range(2):
            keep = (lane >= half * HD) & (lane < (half + 1) * HD)
            q_head = jnp.where(keep, q_pair, jnp.zeros_like(q_pair))
            s = lax.dot_general(
                q_head, keys, (((1,), (1,)), ((), ())), preferred_element_type=jnp.float32
            ) * (1.0 / HD**0.5)
            e = jnp.exp(s - s.max(axis=1, keepdims=True))
            inv = 1.0 / e.sum(axis=1, keepdims=True)
            probs = (e * inv).astype(jnp.bfloat16)
            mixed.append(jnp.dot(probs, vals, preferred_element_type=jnp.float32))
        out = jnp.where(lane < HD, mixed[0], mixed[1])
        out_ref[:, cols] = out.astype(out_ref.dtype)


def per_device(features, gain_attn, w_qkv, w_out, gain_mlp, w_up, w_down, neighbours):
    row_count = features.shape[0]
    patches_here = row_count // PN
    width = w_qkv.shape[2]
    heads_here = width // HD
    n_win = 2 * REACH + 1
    normed = normalize(features, gain_attn)
    w_all = jnp.concatenate([w_qkv[0], w_qkv[1], w_qkv[2]], axis=1)
    qkv = jnp.dot(normed, w_all, preferred_element_type=jnp.float32).astype(jnp.bfloat16)
    queries = qkv[:, :width]
    own_kv = qkv[:, width:]
    window = {0: own_kv}
    for offset in range(-REACH, REACH + 1):
        if offset != 0:
            window[offset] = from_behind(own_kv, "patch", -offset)
    device = lax.axis_index("patch")
    n_dev = lax.axis_size("patch")
    listed = lax.dynamic_slice_in_dim(neighbours, device * patches_here, patches_here, 0)
    owner_dev = listed // patches_here
    offset_dev = jnp.mod(owner_dev - device + n_dev // 2, n_dev) - n_dev // 2
    slot_index = (offset_dev + REACH) * patches_here + jnp.mod(listed, patches_here)
    kv_list = [window[offset] for offset in range(-REACH, REACH + 1)]
    n_mp = lax.axis_size("mp")
    col_width = D // n_mp
    col_begin = lax.axis_index("mp") * col_width
    gain_cols = lax.dynamic_slice_in_dim(gain_mlp, col_begin, col_width, 0)
    feature_cols = lax.dynamic_slice_in_dim(features, col_begin, col_width, 1)
    chunk_patches = patches_here // N_CHUNK
    chunk_rows = chunk_patches * PN
    outs = []
    for chunk in range(N_CHUNK):
        first = chunk * chunk_patches
        kv_spec = pl.BlockSpec((row_count, 2 * width), lambda p, slots: (0, 0))
        attended = pl.pallas_call(
            functools.partial(window_attention, n_heads=heads_here, n_win=n_win, n_nb=K_NB),
            grid_spec=pltpu.PrefetchScalarGridSpec(
                num_scalar_prefetch=1,
                grid=(chunk_patches,),
                in_specs=[pl.BlockSpec((PN, width), lambda p, slots, f=first: (p + f, 0))]
                + [kv_spec] * n_win,
                out_specs=pl.BlockSpec((PN, width), lambda p, slots: (p, 0)),
                scratch_shapes=[pltpu.VMEM((K_NB * PN, 2 * width), jnp.bfloat16)],
            ),
            out_shape=jax.ShapeDtypeStruct((chunk_rows, width), jnp.bfloat16),
        )(slot_index[first:first + chunk_patches].astype(jnp.int32), queries, *kv_list)
        rows = slice(chunk * chunk_rows, (chunk + 1) * chunk_rows)
        outs.append(mlp_part(attended, feature_cols[rows], gain_cols, w_out, w_up, w_down, n_mp))
    return jnp.concatenate(outs, axis=0)


def mlp_part(attended, feature_cols, gain_cols, w_out, w_up, w_down, n_mp):
    partial_value = jnp.dot(attended, w_out, preferred_element_type=jnp.float32)
    col_share = scatter_sum(partial_value.astype(jnp.bfloat16), n_mp)
    residual_cols = feature_cols.astype(jnp.float32) + col_share
    square_sum = gather_sum(jnp.sum(residual_cols * residual_cols, axis=1), n_mp)
    inverse_rms = lax.rsqrt(square_sum / D + 1e-05)
    normed_cols = (residual_cols * inverse_rms[:, None] * gain_cols).astype(jnp.bfloat16)
    normed2 = gather_cols(normed_cols, n_mp)
    hidden = jax.nn.gelu(
        jnp.dot(normed2, w_up, preferred_element_type=jnp.float32), approximate=True
    ).astype(jnp.bfloat16)
    down_term = jnp.dot(hidden, w_down, preferred_element_type=jnp.float32)
    down_cols = scatter_sum(down_term.astype(jnp.bfloat16), n_mp)
    return (residual_cols + down_cols).astype(jnp.bfloat16)


def solution(mesh):
    return jax.shard_map(
        per_device,
        mesh=mesh,
        in_specs=(
            P("patch", None),
            P(),
            P(None, None, "mp"),
            P("mp", None),
            P(),
            P(None, "mp"),
            P("mp", None),
            P(),
        ),
        out_specs=P("patch", "mp"),
        check_vma=False,
    )
```

```python
import functools

import jax
import jax.numpy as jnp
from jax import lax
from jax.experimental import pallas as pl
from jax.experimental.pallas import tpu as pltpu
from jax.sharding import PartitionSpec as P

D = 1024
HD = 64
PN = 128
K_NB = 8
REACH = 2


def from_behind(array, axis, by):
    length = lax.axis_size(axis)
    return lax.ppermute(array, axis, [(i, (i + by) % length) for i in range(length)])


def normalize(rows, gain):
    rows32 = rows.astype(jnp.float32)
    mean_sq = jnp.mean(rows32 * rows32, axis=-1, keepdims=True)
    return (rows32 * lax.rsqrt(mean_sq + 1e-05) * gain).astype(jnp.bfloat16)


def scatter_sum(parts):
    got = lax.all_to_all(parts, "mp", 0, 0)
    total = got[0].astype(jnp.float32)
    for which in range(1, got.shape[0]):
        total = total + got[which].astype(jnp.float32)
    return total


def gather_sum(vector, n_mp):
    got = lax.all_to_all(jnp.broadcast_to(vector[None], (n_mp,) + vector.shape), "mp", 0, 0)
    total = got[0]
    for which in range(1, n_mp):
        total = total + got[which]
    return total


def gather_blocks(block, n_mp):
    return lax.all_to_all(jnp.broadcast_to(block[None], (n_mp,) + block.shape), "mp", 0, 0)


def split_dot(left, weight, n_mp):
    return jnp.einsum(
        "rk,kjc->jrc", left, weight.reshape(weight.shape[0], n_mp, -1),
        preferred_element_type=jnp.float32,
    ).astype(jnp.bfloat16)


def window_attention(slot_ref, query_ref, *refs, n_heads, n_win, n_nb):
    kv_refs, out_ref, gathered = refs[:n_win], refs[n_win], refs[n_win + 1]
    width = n_heads * HD
    per_win = kv_refs[0].shape[0] // PN
    patch = pl.program_id(0)
    for k in range(n_nb):
        slot = slot_ref[patch, k]
        block = slot // per_win
        local = slot % per_win
        for w in range(n_win):
            @pl.when(block == w)
            def _():
                gathered[k * PN:(k + 1) * PN, :] = kv_refs[w][pl.ds(pl.multiple_of(local * PN, PN), PN), :]
    lane = lax.broadcasted_iota(jnp.int32, (PN, 2 * HD), 1)
    for pair in range(n_heads // 2):
        cols = slice(pair * 2 * HD, (pair + 1) * 2 * HD)
        v_cols = slice(width + pair * 2 * HD, width + (pair + 1) * 2 * HD)
        q_pair = query_ref[:, cols]
        keys = gathered[:, cols]
        vals = gathered[:, v_cols]
        mixed = []
        for half in range(2):
            keep = (lane >= half * HD) & (lane < (half + 1) * HD)
            q_head = jnp.where(keep, q_pair, jnp.zeros_like(q_pair))
            s = lax.dot_general(
                q_head, keys, (((1,), (1,)), ((), ())), preferred_element_type=jnp.float32
            ) * (1.0 / HD**0.5)
            e = jnp.exp(s - s.max(axis=1, keepdims=True))
            inv = 1.0 / e.sum(axis=1, keepdims=True)
            probs = (e * inv).astype(jnp.bfloat16)
            mixed.append(jnp.dot(probs, vals, preferred_element_type=jnp.float32))
        out = jnp.where(lane < HD, mixed[0], mixed[1])
        out_ref[:, cols] = out.astype(out_ref.dtype)


def per_device(features, gain_attn, w_qkv, w_out, gain_mlp, w_up, w_down, neighbours):
    row_count = features.shape[0]
    patches_here = row_count // PN
    width = w_qkv.shape[2]
    heads_here = width // HD
    n_win = 2 * REACH + 1
    normed = normalize(features, gain_attn)
    w_all = jnp.concatenate([w_qkv[0], w_qkv[1], w_qkv[2]], axis=1)
    qkv = jnp.dot(normed, w_all, preferred_element_type=jnp.float32).astype(jnp.bfloat16)
    queries = qkv[:, :width]
    own_kv = qkv[:, width:]
    window = {0: own_kv}
    for offset in range(-REACH, REACH + 1):
        if offset != 0:
            window[offset] = from_behind(own_kv, "patch", -offset)
    device = lax.axis_index("patch")
    n_dev = lax.axis_size("patch")
    listed = lax.dynamic_slice_in_dim(neighbours, device * patches_here, patches_here, 0)
    owner_dev = listed // patches_here
    offset_dev = jnp.mod(owner_dev - device + n_dev // 2, n_dev) - n_dev // 2
    slot_index = (offset_dev + REACH) * patches_here + jnp.mod(listed, patches_here)
    kv_list = [window[offset] for offset in range(-REACH, REACH + 1)]
    kv_spec = pl.BlockSpec((row_count, 2 * width), lambda p, slots: (0, 0))
    attended = pl.pallas_call(
        functools.partial(window_attention, n_heads=heads_here, n_win=n_win, n_nb=K_NB),
        grid_spec=pltpu.PrefetchScalarGridSpec(
            num_scalar_prefetch=1,
            grid=(patches_here,),
            in_specs=[pl.BlockSpec((PN, width), lambda p, slots: (p, 0))] + [kv_spec] * n_win,
            out_specs=pl.BlockSpec((PN, width), lambda p, slots: (p, 0)),
            scratch_shapes=[pltpu.VMEM((K_NB * PN, 2 * width), jnp.bfloat16)],
        ),
        out_shape=jax.ShapeDtypeStruct((row_count, width), jnp.bfloat16),
    )(slot_index.astype(jnp.int32), queries, *kv_list)
    n_mp = lax.axis_size("mp")
    col_share = scatter_sum(split_dot(attended, w_out, n_mp))
    col_width = col_share.shape[1]
    col_begin = lax.axis_index("mp") * col_width
    residual_cols = (
        lax.dynamic_slice_in_dim(features, col_begin, col_width, 1).astype(jnp.float32) + col_share
    )
    gain_cols = lax.dynamic_slice_in_dim(gain_mlp, col_begin, col_width, 0)
    square_sum = gather_sum(jnp.sum(residual_cols * residual_cols, axis=1), n_mp)
    inverse_rms = lax.rsqrt(square_sum / D + 1e-05)
    normed_cols = (residual_cols * inverse_rms[:, None] * gain_cols).astype(jnp.bfloat16)
    normed2 = gather_blocks(normed_cols, n_mp)
    up = jnp.einsum(
        "jrc,jch->rh", normed2, w_up.reshape(n_mp, col_width, -1),
        preferred_element_type=jnp.float32,
    )
    hidden = jax.nn.gelu(up, approximate=True).astype(jnp.bfloat16)
    down_cols = scatter_sum(split_dot(hidden, w_down, n_mp))
    return (residual_cols + down_cols).astype(jnp.bfloat16)


def solution(mesh):
    return jax.shard_map(
        per_device,
        mesh=mesh,
        in_specs=(
            P("patch", None),
            P(),
            P(None, None, "mp"),
            P("mp", None),
            P(),
            P(None, "mp"),
            P("mp", None),
            P(),
        ),
        out_specs=P("patch", "mp"),
        check_vma=False,
    )
```

```python
import functools

import jax
import jax.numpy as jnp
from jax import lax
from jax.experimental import pallas as pl
from jax.experimental.pallas import tpu as pltpu
from jax.sharding import PartitionSpec as P

D = 1024
HD = 64
PN = 128
K_NB = 8
REACH = 2


def from_behind(array, axis, by):
    length = lax.axis_size(axis)
    return lax.ppermute(array, axis, [(i, (i + by) % length) for i in range(length)])


def normalize(rows, gain):
    rows32 = rows.astype(jnp.float32)
    mean_sq = jnp.mean(rows32 * rows32, axis=-1, keepdims=True)
    return (rows32 * lax.rsqrt(mean_sq + 1e-05) * gain).astype(jnp.bfloat16)


def scatter_sum(parts, n_mp):
    rows, cols = parts.shape
    got = lax.all_to_all(parts.reshape(rows, n_mp, cols // n_mp), "mp", 1, 1)
    total = got[:, 0].astype(jnp.float32)
    for which in range(1, n_mp):
        total = total + got[:, which].astype(jnp.float32)
    return total


def gather_sum(vector, n_mp):
    got = lax.all_to_all(jnp.broadcast_to(vector[None], (n_mp,) + vector.shape), "mp", 0, 0)
    total = got[0]
    for which in range(1, n_mp):
        total = total + got[which]
    return total


def gather_cols(block, n_mp):
    rows, cols = block.shape
    spread = jnp.broadcast_to(block[:, None], (rows, n_mp, cols))
    return lax.all_to_all(spread, "mp", 1, 1).reshape(rows, n_mp * cols)


def window_attention(slot_ref, query_ref, *refs, n_heads, n_win, n_nb):
    kv_refs, out_ref, gathered = refs[:n_win], refs[n_win], refs[n_win + 1]
    width = n_heads * HD
    per_win = kv_refs[0].shape[0] // PN
    patch = pl.program_id(0)
    for k in range(n_nb):
        slot = slot_ref[patch, k]
        block = slot // per_win
        local = slot % per_win
        for w in range(n_win):
            @pl.when(block == w)
            def _():
                gathered[k * PN:(k + 1) * PN, :] = kv_refs[w][pl.ds(pl.multiple_of(local * PN, PN), PN), :]
    lane = lax.broadcasted_iota(jnp.int32, (PN, 2 * HD), 1)
    for pair in range(n_heads // 2):
        cols = slice(pair * 2 * HD, (pair + 1) * 2 * HD)
        v_cols = slice(width + pair * 2 * HD, width + (pair + 1) * 2 * HD)
        q_pair = query_ref[:, cols]
        keys = gathered[:, cols]
        vals = gathered[:, v_cols]
        mixed = []
        for half in range(2):
            keep = (lane >= half * HD) & (lane < (half + 1) * HD)
            q_head = jnp.where(keep, q_pair, jnp.zeros_like(q_pair))
            s = lax.dot_general(
                q_head, keys, (((1,), (1,)), ((), ())), preferred_element_type=jnp.float32
            ) * (1.0 / HD**0.5)
            e = jnp.exp(s - s.max(axis=1, keepdims=True))
            inv = 1.0 / e.sum(axis=1, keepdims=True)
            probs = (e * inv).astype(jnp.bfloat16)
            mixed.append(jnp.dot(probs, vals, preferred_element_type=jnp.float32))
        out = jnp.where(lane < HD, mixed[0], mixed[1])
        out_ref[:, cols] = out.astype(out_ref.dtype)


def per_device(features, gain_attn, w_qkv, w_out, gain_mlp, w_up, w_down, neighbours):
    row_count = features.shape[0]
    patches_here = row_count // PN
    width = w_qkv.shape[2]
    heads_here = width // HD
    n_win = 2 * REACH + 1
    normed = normalize(features, gain_attn)
    w_all = jnp.concatenate([w_qkv[0], w_qkv[1], w_qkv[2]], axis=1)
    qkv = jnp.dot(normed, w_all, preferred_element_type=jnp.float32).astype(jnp.bfloat16)
    queries = qkv[:, :width]
    own_kv = qkv[:, width:]
    device = lax.axis_index("patch")
    n_dev = lax.axis_size("patch")
    core = device % 2
    from_before = from_behind(own_kv, "patch", 2)
    from_after = from_behind(own_kv, "patch", -2)
    partner = lax.ppermute(own_kv, "patch", [(i, i ^ 1) for i in range(n_dev)])
    relay = jnp.where(core == 0, from_after, from_before)
    relayed = lax.ppermute(relay, "patch", [(i, i ^ 1) for i in range(n_dev)])
    kv_list = [from_before, partner, own_kv, relayed, from_after]
    listed = lax.dynamic_slice_in_dim(neighbours, device * patches_here, patches_here, 0)
    owner_dev = listed // patches_here
    offset_dev = jnp.mod(owner_dev - device + n_dev // 2, n_dev) - n_dev // 2
    block = offset_dev + REACH
    swap = (core == 0) & ((offset_dev == 1) | (offset_dev == -1))
    block = jnp.where(swap, 4 - block, block)
    slot_index = block * patches_here + jnp.mod(listed, patches_here)
    kv_spec = pl.BlockSpec((row_count, 2 * width), lambda p, slots: (0, 0))
    attended = pl.pallas_call(
        functools.partial(window_attention, n_heads=heads_here, n_win=n_win, n_nb=K_NB),
        grid_spec=pltpu.PrefetchScalarGridSpec(
            num_scalar_prefetch=1,
            grid=(patches_here,),
            in_specs=[pl.BlockSpec((PN, width), lambda p, slots: (p, 0))] + [kv_spec] * n_win,
            out_specs=pl.BlockSpec((PN, width), lambda p, slots: (p, 0)),
            scratch_shapes=[pltpu.VMEM((K_NB * PN, 2 * width), jnp.bfloat16)],
        ),
        out_shape=jax.ShapeDtypeStruct((row_count, width), jnp.bfloat16),
    )(slot_index.astype(jnp.int32), queries, *kv_list)
    n_mp = lax.axis_size("mp")
    partial_value = jnp.dot(attended, w_out, preferred_element_type=jnp.float32)
    col_share = scatter_sum(partial_value.astype(jnp.bfloat16), n_mp)
    col_width = col_share.shape[1]
    col_begin = lax.axis_index("mp") * col_width
    residual_cols = (
        lax.dynamic_slice_in_dim(features, col_begin, col_width, 1).astype(jnp.float32) + col_share
    )
    gain_cols = lax.dynamic_slice_in_dim(gain_mlp, col_begin, col_width, 0)
    square_sum = gather_sum(jnp.sum(residual_cols * residual_cols, axis=1), n_mp)
    inverse_rms = lax.rsqrt(square_sum / D + 1e-05)
    normed_cols = (residual_cols * inverse_rms[:, None] * gain_cols).astype(jnp.bfloat16)
    normed2 = gather_cols(normed_cols, n_mp)
    hidden = jax.nn.gelu(
        jnp.dot(normed2, w_up, preferred_element_type=jnp.float32), approximate=True
    ).astype(jnp.bfloat16)
    down_term = jnp.dot(hidden, w_down, preferred_element_type=jnp.float32)
    down_cols = scatter_sum(down_term.astype(jnp.bfloat16), n_mp)
    return (residual_cols + down_cols).astype(jnp.bfloat16)


def solution(mesh):
    return jax.shard_map(
        per_device,
        mesh=mesh,
        in_specs=(
            P("patch", None),
            P(),
            P(None, None, "mp"),
            P("mp", None),
            P(),
            P(None, "mp"),
            P("mp", None),
            P(),
        ),
        out_specs=P("patch", "mp"),
        check_vma=False,
    )
```

```python
import functools

import jax
import jax.numpy as jnp
from jax import lax
from jax.experimental import pallas as pl
from jax.experimental.pallas import tpu as pltpu
from jax.sharding import PartitionSpec as P

D = 1024
HD = 64
PN = 128
K_NB = 8
REACH = 2


def from_behind(array, axis, by):
    length = lax.axis_size(axis)
    return lax.ppermute(array, axis, [(i, (i + by) % length) for i in range(length)])


def normalize(rows, gain):
    rows32 = rows.astype(jnp.float32)
    mean_sq = jnp.mean(rows32 * rows32, axis=-1, keepdims=True)
    return (rows32 * lax.rsqrt(mean_sq + 1e-05) * gain).astype(jnp.bfloat16)


def scatter_sum(parts, n_mp):
    rows, cols = parts.shape
    got = lax.all_to_all(parts.reshape(rows, n_mp, cols // n_mp), "mp", 1, 1)
    total = got[:, 0].astype(jnp.float32)
    for which in range(1, n_mp):
        total = total + got[:, which].astype(jnp.float32)
    return total


def gather_cols(block, n_mp):
    rows, cols = block.shape
    spread = jnp.broadcast_to(block[:, None], (rows, n_mp, cols))
    return lax.all_to_all(spread, "mp", 1, 1).reshape(rows, n_mp * cols)


def window_attention(slot_ref, query_ref, *refs, n_heads, n_win, n_nb):
    kv_refs, out_ref, gathered = refs[:n_win], refs[n_win], refs[n_win + 1]
    width = n_heads * HD
    per_win = kv_refs[0].shape[0] // PN
    patch = pl.program_id(0)
    for k in range(n_nb):
        slot = slot_ref[patch, k]
        block = slot // per_win
        local = slot % per_win
        for w in range(n_win):
            @pl.when(block == w)
            def _():
                gathered[k * PN:(k + 1) * PN, :] = kv_refs[w][pl.ds(pl.multiple_of(local * PN, PN), PN), :]
    lane = lax.broadcasted_iota(jnp.int32, (PN, 2 * HD), 1)
    for pair in range(n_heads // 2):
        cols = slice(pair * 2 * HD, (pair + 1) * 2 * HD)
        v_cols = slice(width + pair * 2 * HD, width + (pair + 1) * 2 * HD)
        q_pair = query_ref[:, cols]
        keys = gathered[:, cols]
        vals = gathered[:, v_cols]
        mixed = []
        for half in range(2):
            keep = (lane >= half * HD) & (lane < (half + 1) * HD)
            q_head = jnp.where(keep, q_pair, jnp.zeros_like(q_pair))
            s = lax.dot_general(
                q_head, keys, (((1,), (1,)), ((), ())), preferred_element_type=jnp.float32
            ) * (1.0 / HD**0.5)
            e = jnp.exp(s - s.max(axis=1, keepdims=True))
            inv = 1.0 / e.sum(axis=1, keepdims=True)
            probs = (e * inv).astype(jnp.bfloat16)
            mixed.append(jnp.dot(probs, vals, preferred_element_type=jnp.float32))
        out = jnp.where(lane < HD, mixed[0], mixed[1])
        out_ref[:, cols] = out.astype(out_ref.dtype)


def per_device(features, gain_attn, w_qkv, w_out, gain_mlp, w_up, w_down, neighbours):
    row_count = features.shape[0]
    patches_here = row_count // PN
    width = w_qkv.shape[2]
    heads_here = width // HD
    n_win = 2 * REACH + 1
    normed = normalize(features, gain_attn)
    w_all = jnp.concatenate([w_qkv[0], w_qkv[1], w_qkv[2]], axis=1)
    qkv = jnp.dot(normed, w_all, preferred_element_type=jnp.float32).astype(jnp.bfloat16)
    queries = qkv[:, :width]
    own_kv = qkv[:, width:]
    window = {0: own_kv}
    for offset in range(-REACH, REACH + 1):
        if offset != 0:
            window[offset] = from_behind(own_kv, "patch", -offset)
    device = lax.axis_index("patch")
    n_dev = lax.axis_size("patch")
    listed = lax.dynamic_slice_in_dim(neighbours, device * patches_here, patches_here, 0)
    owner_dev = listed // patches_here
    offset_dev = jnp.mod(owner_dev - device + n_dev // 2, n_dev) - n_dev // 2
    slot_index = (offset_dev + REACH) * patches_here + jnp.mod(listed, patches_here)
    kv_list = [window[offset] for offset in range(-REACH, REACH + 1)]
    kv_spec = pl.BlockSpec((row_count, 2 * width), lambda p, slots: (0, 0))
    attended = pl.pallas_call(
        functools.partial(window_attention, n_heads=heads_here, n_win=n_win, n_nb=K_NB),
        grid_spec=pltpu.PrefetchScalarGridSpec(
            num_scalar_prefetch=1,
            grid=(patches_here,),
            in_specs=[pl.BlockSpec((PN, width), lambda p, slots: (p, 0))] + [kv_spec] * n_win,
            out_specs=pl.BlockSpec((PN, width), lambda p, slots: (p, 0)),
            scratch_shapes=[pltpu.VMEM((K_NB * PN, 2 * width), jnp.bfloat16)],
        ),
        out_shape=jax.ShapeDtypeStruct((row_count, width), jnp.bfloat16),
    )(slot_index.astype(jnp.int32), queries, *kv_list)
    n_mp = lax.axis_size("mp")
    partial_value = jnp.dot(attended, w_out, preferred_element_type=jnp.float32)
    col_share = scatter_sum(partial_value.astype(jnp.bfloat16), n_mp)
    col_width = col_share.shape[1]
    col_begin = lax.axis_index("mp") * col_width
    residual_cols = (
        lax.dynamic_slice_in_dim(features, col_begin, col_width, 1).astype(jnp.float32) + col_share
    )
    rows_full = gather_cols(residual_cols.astype(jnp.bfloat16), n_mp).astype(jnp.float32)
    square_sum = jnp.sum(rows_full * rows_full, axis=1, keepdims=True)
    inverse_rms = lax.rsqrt(square_sum / D + 1e-05)
    normed2 = (rows_full * inverse_rms * gain_mlp).astype(jnp.bfloat16)
    hidden = jax.nn.gelu(
        jnp.dot(normed2, w_up, preferred_element_type=jnp.float32), approximate=True
    ).astype(jnp.bfloat16)
    down_term = jnp.dot(hidden, w_down, preferred_element_type=jnp.float32)
    down_cols = scatter_sum(down_term.astype(jnp.bfloat16), n_mp)
    return (residual_cols + down_cols).astype(jnp.bfloat16)


def solution(mesh):
    return jax.shard_map(
        per_device,
        mesh=mesh,
        in_specs=(
            P("patch", None),
            P(),
            P(None, None, "mp"),
            P("mp", None),
            P(),
            P(None, "mp"),
            P("mp", None),
            P(),
        ),
        out_specs=P("patch", "mp"),
        check_vma=False,
    )
```

```python
import functools

import jax
import jax.numpy as jnp
from jax import lax
from jax.experimental import pallas as pl
from jax.experimental.pallas import tpu as pltpu
from jax.sharding import PartitionSpec as P

D = 1024
HD = 64
PN = 128
K_NB = 8
REACH = 2


def from_behind(array, axis, by):
    length = lax.axis_size(axis)
    return lax.ppermute(array, axis, [(i, (i + by) % length) for i in range(length)])


def normalize(rows, gain):
    rows32 = rows.astype(jnp.float32)
    mean_sq = jnp.mean(rows32 * rows32, axis=-1, keepdims=True)
    return (rows32 * lax.rsqrt(mean_sq + 1e-05) * gain).astype(jnp.bfloat16)


def scatter_sum(parts, n_mp):
    rows, cols = parts.shape
    got = lax.all_to_all(parts.reshape(rows, n_mp, cols // n_mp), "mp", 1, 1)
    total = got[:, 0].astype(jnp.float32)
    for which in range(1, n_mp):
        total = total + got[:, which].astype(jnp.float32)
    return total


def gather_sum(vector, n_mp):
    got = lax.all_to_all(jnp.broadcast_to(vector[None], (n_mp,) + vector.shape), "mp", 0, 0)
    total = got[0]
    for which in range(1, n_mp):
        total = total + got[which]
    return total


def gather_cols(block, n_mp):
    rows, cols = block.shape
    spread = jnp.broadcast_to(block[:, None], (rows, n_mp, cols))
    return lax.all_to_all(spread, "mp", 1, 1).reshape(rows, n_mp * cols)


def window_attention(slot_ref, query_ref, *refs, n_heads, n_win, n_nb):
    kv_refs, out_ref, gathered = refs[:n_win], refs[n_win], refs[n_win + 1]
    per_win = kv_refs[0].shape[1] // PN
    patch = pl.program_id(0)
    for k in range(n_nb):
        slot = slot_ref[patch, k]
        block = slot // per_win
        local = slot % per_win
        for w in range(n_win):
            @pl.when(block == w)
            def _():
                start = pl.multiple_of(local * PN, PN)
                gathered[:, k * PN:(k + 1) * PN, :] = kv_refs[w][:, pl.ds(start, PN), :]
    lane = lax.broadcasted_iota(jnp.int32, (PN, 2 * HD), 1)
    for pair in range(n_heads // 2):
        cols = slice(pair * 2 * HD, (pair + 1) * 2 * HD)
        q_pair = query_ref[:, cols] * jnp.asarray(1.0 / HD**0.5, query_ref.dtype)
        keys = gathered[0, :, cols]
        vals = gathered[1, :, cols]
        mixed = []
        for half in range(2):
            keep = (lane >= half * HD) & (lane < (half + 1) * HD)
            q_head = jnp.where(keep, q_pair, jnp.zeros_like(q_pair))
            s = lax.dot_general(
                q_head, keys, (((1,), (1,)), ((), ())), preferred_element_type=jnp.float32
            )
            e = jnp.exp(s - s.max(axis=1, keepdims=True))
            inv = 1.0 / e.sum(axis=1, keepdims=True)
            probs = (e * inv).astype(jnp.bfloat16)
            mixed.append(jnp.dot(probs, vals, preferred_element_type=jnp.float32))
        out = jnp.where(lane < HD, mixed[0], mixed[1])
        out_ref[:, cols] = out.astype(out_ref.dtype)


def per_device(features, gain_attn, w_qkv, w_out, gain_mlp, w_up, w_down, neighbours):
    row_count = features.shape[0]
    patches_here = row_count // PN
    width = w_qkv.shape[2]
    heads_here = width // HD
    n_win = 2 * REACH + 1
    normed = normalize(features, gain_attn)
    qkv = jnp.einsum(
        "rk,tkc->trc", normed, w_qkv, preferred_element_type=jnp.float32
    ).astype(jnp.bfloat16)
    queries = qkv[0]
    own_kv = qkv[1:]
    window = {0: own_kv}
    for offset in range(-REACH, REACH + 1):
        if offset != 0:
            window[offset] = from_behind(own_kv, "patch", -offset)
    device = lax.axis_index("patch")
    n_dev = lax.axis_size("patch")
    listed = lax.dynamic_slice_in_dim(neighbours, device * patches_here, patches_here, 0)
    owner_dev = listed // patches_here
    offset_dev = jnp.mod(owner_dev - device + n_dev // 2, n_dev) - n_dev // 2
    slot_index = (offset_dev + REACH) * patches_here + jnp.mod(listed, patches_here)
    kv_list = [window[offset] for offset in range(-REACH, REACH + 1)]
    kv_spec = pl.BlockSpec((2, row_count, width), lambda p, slots: (0, 0, 0))
    attended = pl.pallas_call(
        functools.partial(window_attention, n_heads=heads_here, n_win=n_win, n_nb=K_NB),
        grid_spec=pltpu.PrefetchScalarGridSpec(
            num_scalar_prefetch=1,
            grid=(patches_here,),
            in_specs=[pl.BlockSpec((PN, width), lambda p, slots: (p, 0))] + [kv_spec] * n_win,
            out_specs=pl.BlockSpec((PN, width), lambda p, slots: (p, 0)),
            scratch_shapes=[pltpu.VMEM((2, K_NB * PN, width), jnp.bfloat16)],
        ),
        out_shape=jax.ShapeDtypeStruct((row_count, width), jnp.bfloat16),
    )(slot_index.astype(jnp.int32), queries, *kv_list)
    n_mp = lax.axis_size("mp")
    partial_value = jnp.dot(attended, w_out, preferred_element_type=jnp.float32)
    col_share = scatter_sum(partial_value.astype(jnp.bfloat16), n_mp)
    col_width = col_share.shape[1]
    col_begin = lax.axis_index("mp") * col_width
    residual_cols = (
        lax.dynamic_slice_in_dim(features, col_begin, col_width, 1).astype(jnp.float32) + col_share
    )
    gain_cols = lax.dynamic_slice_in_dim(gain_mlp, col_begin, col_width, 0)
    square_sum = gather_sum(jnp.sum(residual_cols * residual_cols, axis=1), n_mp)
    inverse_rms = lax.rsqrt(square_sum / D + 1e-05)
    normed_cols = (residual_cols * inverse_rms[:, None] * gain_cols).astype(jnp.bfloat16)
    normed2 = gather_cols(normed_cols, n_mp)
    hidden = jax.nn.gelu(
        jnp.dot(normed2, w_up, preferred_element_type=jnp.float32), approximate=True
    ).astype(jnp.bfloat16)
    down_term = jnp.dot(hidden, w_down, preferred_element_type=jnp.float32)
    down_cols = scatter_sum(down_term.astype(jnp.bfloat16), n_mp)
    return (residual_cols + down_cols).astype(jnp.bfloat16)


def solution(mesh):
    return jax.shard_map(
        per_device,
        mesh=mesh,
        in_specs=(
            P("patch", None),
            P(),
            P(None, None, "mp"),
            P("mp", None),
            P(),
            P(None, "mp"),
            P("mp", None),
            P(),
        ),
        out_specs=P("patch", "mp"),
        check_vma=False,
    )
```

```python
import functools

import jax
import jax.numpy as jnp
from jax import lax
from jax.experimental import pallas as pl
from jax.experimental.pallas import tpu as pltpu
from jax.sharding import PartitionSpec as P

D = 1024
HD = 64
PN = 128
K_NB = 8
REACH = 2


def from_behind(array, axis, by):
    length = lax.axis_size(axis)
    return lax.ppermute(array, axis, [(i, (i + by) % length) for i in range(length)])


def normalize(rows, gain):
    rows32 = rows.astype(jnp.float32)
    mean_sq = jnp.mean(rows32 * rows32, axis=-1, keepdims=True)
    return (rows32 * lax.rsqrt(mean_sq + 1e-05) * gain).astype(jnp.bfloat16)


def scatter_sum(parts):
    got = lax.all_to_all(parts, "mp", 0, 0)
    total = got[0].astype(jnp.float32)
    for which in range(1, got.shape[0]):
        total = total + got[which].astype(jnp.float32)
    return total


def scatter_cols(parts, n_mp):
    rows, cols = parts.shape
    return scatter_sum(parts.reshape(rows, n_mp, cols // n_mp).transpose(1, 0, 2))


def gather_sum(vector, n_mp):
    got = lax.all_to_all(jnp.broadcast_to(vector[None], (n_mp,) + vector.shape), "mp", 0, 0)
    total = got[0]
    for which in range(1, n_mp):
        total = total + got[which]
    return total


def gather_cols(block, n_mp):
    rows, cols = block.shape
    spread = jnp.broadcast_to(block[:, None], (rows, n_mp, cols))
    return lax.all_to_all(spread, "mp", 1, 1).reshape(rows, n_mp * cols)


def window_attention(slot_ref, query_ref, *refs, n_heads, n_win, n_nb):
    kv_refs, w_ref, out_ref = refs[:n_win], refs[n_win], refs[n_win + 1]
    mixed_ref, gathered = refs[n_win + 2], refs[n_win + 3]
    width = n_heads * HD
    per_win = kv_refs[0].shape[0] // PN
    patch = pl.program_id(0)
    for k in range(n_nb):
        slot = slot_ref[patch, k]
        block = slot // per_win
        local = slot % per_win
        for w in range(n_win):
            @pl.when(block == w)
            def _():
                gathered[k * PN:(k + 1) * PN, :] = kv_refs[w][pl.ds(pl.multiple_of(local * PN, PN), PN), :]
    lane = lax.broadcasted_iota(jnp.int32, (PN, 2 * HD), 1)
    for pair in range(n_heads // 2):
        cols = slice(pair * 2 * HD, (pair + 1) * 2 * HD)
        v_cols = slice(width + pair * 2 * HD, width + (pair + 1) * 2 * HD)
        q_pair = query_ref[:, cols]
        keys = gathered[:, cols]
        vals = gathered[:, v_cols]
        mixed = []
        for half in range(2):
            keep = (lane >= half * HD) & (lane < (half + 1) * HD)
            q_head = jnp.where(keep, q_pair, jnp.zeros_like(q_pair))
            s = lax.dot_general(
                q_head, keys, (((1,), (1,)), ((), ())), preferred_element_type=jnp.float32
            ) * (1.0 / HD**0.5)
            e = jnp.exp(s - s.max(axis=1, keepdims=True))
            inv = 1.0 / e.sum(axis=1, keepdims=True)
            probs = (e * inv).astype(jnp.bfloat16)
            mixed.append(jnp.dot(probs, vals, preferred_element_type=jnp.float32))
        out = jnp.where(lane < HD, mixed[0], mixed[1])
        mixed_ref[:, cols] = out.astype(mixed_ref.dtype)
    projected = jnp.dot(mixed_ref[...], w_ref[...], preferred_element_type=jnp.float32)
    chunk = out_ref.shape[2]
    for j in range(out_ref.shape[0]):
        out_ref[j] = projected[:, j * chunk:(j + 1) * chunk].astype(out_ref.dtype)


def per_device(features, gain_attn, w_qkv, w_out, gain_mlp, w_up, w_down, neighbours):
    row_count = features.shape[0]
    patches_here = row_count // PN
    width = w_qkv.shape[2]
    heads_here = width // HD
    n_win = 2 * REACH + 1
    normed = normalize(features, gain_attn)
    w_all = jnp.concatenate([w_qkv[0], w_qkv[1], w_qkv[2]], axis=1)
    qkv = jnp.dot(normed, w_all, preferred_element_type=jnp.float32).astype(jnp.bfloat16)
    queries = qkv[:, :width]
    own_kv = qkv[:, width:]
    window = {0: own_kv}
    for offset in range(-REACH, REACH + 1):
        if offset != 0:
            window[offset] = from_behind(own_kv, "patch", -offset)
    device = lax.axis_index("patch")
    n_dev = lax.axis_size("patch")
    listed = lax.dynamic_slice_in_dim(neighbours, device * patches_here, patches_here, 0)
    owner_dev = listed // patches_here
    offset_dev = jnp.mod(owner_dev - device + n_dev // 2, n_dev) - n_dev // 2
    slot_index = (offset_dev + REACH) * patches_here + jnp.mod(listed, patches_here)
    kv_list = [window[offset] for offset in range(-REACH, REACH + 1)]
    n_mp = lax.axis_size("mp")
    kv_spec = pl.BlockSpec((row_count, 2 * width), lambda p, slots: (0, 0))
    partial_value = pl.pallas_call(
        functools.partial(window_attention, n_heads=heads_here, n_win=n_win, n_nb=K_NB),
        grid_spec=pltpu.PrefetchScalarGridSpec(
            num_scalar_prefetch=1,
            grid=(patches_here,),
            in_specs=[pl.BlockSpec((PN, width), lambda p, slots: (p, 0))]
            + [kv_spec] * n_win
            + [pl.BlockSpec((width, D), lambda p, slots: (0, 0))],
            out_specs=pl.BlockSpec((n_mp, PN, D // n_mp), lambda p, slots: (0, p, 0)),
            scratch_shapes=[
                pltpu.VMEM((PN, width), jnp.bfloat16),
                pltpu.VMEM((K_NB * PN, 2 * width), jnp.bfloat16),
            ],
        ),
        out_shape=jax.ShapeDtypeStruct((n_mp, row_count, D // n_mp), jnp.bfloat16),
    )(slot_index.astype(jnp.int32), queries, *kv_list, w_out)
    col_share = scatter_sum(partial_value)
    col_width = col_share.shape[1]
    col_begin = lax.axis_index("mp") * col_width
    residual_cols = (
        lax.dynamic_slice_in_dim(features, col_begin, col_width, 1).astype(jnp.float32) + col_share
    )
    gain_cols = lax.dynamic_slice_in_dim(gain_mlp, col_begin, col_width, 0)
    square_sum = gather_sum(jnp.sum(residual_cols * residual_cols, axis=1), n_mp)
    inverse_rms = lax.rsqrt(square_sum / D + 1e-05)
    normed_cols = (residual_cols * inverse_rms[:, None] * gain_cols).astype(jnp.bfloat16)
    normed2 = gather_cols(normed_cols, n_mp)
    hidden = jax.nn.gelu(
        jnp.dot(normed2, w_up, preferred_element_type=jnp.float32), approximate=True
    ).astype(jnp.bfloat16)
    down_term = jnp.dot(hidden, w_down, preferred_element_type=jnp.float32)
    down_cols = scatter_cols(down_term.astype(jnp.bfloat16), n_mp)
    return (residual_cols + down_cols).astype(jnp.bfloat16)


def solution(mesh):
    return jax.shard_map(
        per_device,
        mesh=mesh,
        in_specs=(
            P("patch", None),
            P(),
            P(None, None, "mp"),
            P("mp", None),
            P(),
            P(None, "mp"),
            P("mp", None),
            P(),
        ),
        out_specs=P("patch", "mp"),
        check_vma=False,
    )
```

```python
import functools

import jax
import jax.numpy as jnp
from jax import lax
from jax.experimental import pallas as pl
from jax.experimental.pallas import tpu as pltpu
from jax.sharding import PartitionSpec as P

D = 1024
HD = 64
PN = 128
K_NB = 8
REACH = 2


def from_behind(array, axis, by):
    length = lax.axis_size(axis)
    return lax.ppermute(array, axis, [(i, (i + by) % length) for i in range(length)])


def normalize(rows, gain):
    rows32 = rows.astype(jnp.float32)
    mean_sq = jnp.mean(rows32 * rows32, axis=-1, keepdims=True)
    return (rows32 * lax.rsqrt(mean_sq + 1e-05) * gain).astype(jnp.bfloat16)


def scatter_sum(parts):
    got = lax.all_to_all(parts, "mp", 0, 0)
    total = got[0].astype(jnp.float32)
    for which in range(1, got.shape[0]):
        total = total + got[which].astype(jnp.float32)
    return total


def scatter_cols(parts, n_mp):
    rows, cols = parts.shape
    got = lax.all_to_all(parts.reshape(rows, n_mp, cols // n_mp), "mp", 1, 1)
    total = got[:, 0].astype(jnp.float32)
    for which in range(1, n_mp):
        total = total + got[:, which].astype(jnp.float32)
    return total


def gather_sum(vector, n_mp):
    got = lax.all_to_all(jnp.broadcast_to(vector[None], (n_mp,) + vector.shape), "mp", 0, 0)
    total = got[0]
    for which in range(1, n_mp):
        total = total + got[which]
    return total


def gather_cols(block, n_mp):
    rows, cols = block.shape
    spread = jnp.broadcast_to(block[:, None], (rows, n_mp, cols))
    return lax.all_to_all(spread, "mp", 1, 1).reshape(rows, n_mp * cols)


def window_attention(slot_ref, query_ref, *refs, n_heads, n_win, n_nb):
    kv_refs, w_ref, out_ref = refs[:n_win], refs[n_win], refs[n_win + 1]
    mixed_ref, gathered = refs[n_win + 2], refs[n_win + 3]
    width = n_heads * HD
    per_win = kv_refs[0].shape[0] // PN
    patch = pl.program_id(0)
    for k in range(n_nb):
        slot = slot_ref[patch, k]
        block = slot // per_win
        local = slot % per_win
        for w in range(n_win):
            @pl.when(block == w)
            def _():
                gathered[k * PN:(k + 1) * PN, :] = kv_refs[w][pl.ds(pl.multiple_of(local * PN, PN), PN), :]
    lane = lax.broadcasted_iota(jnp.int32, (PN, 2 * HD), 1)
    for pair in range(n_heads // 2):
        cols = slice(pair * 2 * HD, (pair + 1) * 2 * HD)
        v_cols = slice(width + pair * 2 * HD, width + (pair + 1) * 2 * HD)
        q_pair = query_ref[:, cols]
        keys = gathered[:, cols]
        vals = gathered[:, v_cols]
        mixed = []
        for half in range(2):
            keep = (lane >= half * HD) & (lane < (half + 1) * HD)
            q_head = jnp.where(keep, q_pair, jnp.zeros_like(q_pair))
            s = lax.dot_general(
                q_head, keys, (((1,), (1,)), ((), ())), preferred_element_type=jnp.float32
            ) * (1.0 / HD**0.5)
            e = jnp.exp(s - s.max(axis=1, keepdims=True))
            inv = 1.0 / e.sum(axis=1, keepdims=True)
            probs = (e * inv).astype(jnp.bfloat16)
            mixed.append(jnp.dot(probs, vals, preferred_element_type=jnp.float32))
        out = jnp.where(lane < HD, mixed[0], mixed[1])
        mixed_ref[:, cols] = out.astype(mixed_ref.dtype)
    projected = jnp.dot(mixed_ref[...], w_ref[...], preferred_element_type=jnp.float32)
    chunk = out_ref.shape[2]
    for j in range(out_ref.shape[0]):
        out_ref[j] = projected[:, j * chunk:(j + 1) * chunk].astype(out_ref.dtype)


def per_device(features, gain_attn, w_qkv, w_out, gain_mlp, w_up, w_down, neighbours):
    row_count = features.shape[0]
    patches_here = row_count // PN
    width = w_qkv.shape[2]
    heads_here = width // HD
    n_win = 2 * REACH + 1
    normed = normalize(features, gain_attn)
    w_all = jnp.concatenate([w_qkv[0], w_qkv[1], w_qkv[2]], axis=1)
    qkv = jnp.dot(normed, w_all, preferred_element_type=jnp.float32).astype(jnp.bfloat16)
    queries = qkv[:, :width]
    own_kv = qkv[:, width:]
    window = {0: own_kv}
    for offset in range(-REACH, REACH + 1):
        if offset != 0:
            window[offset] = from_behind(own_kv, "patch", -offset)
    device = lax.axis_index("patch")
    n_dev = lax.axis_size("patch")
    listed = lax.dynamic_slice_in_dim(neighbours, device * patches_here, patches_here, 0)
    owner_dev = listed // patches_here
    offset_dev = jnp.mod(owner_dev - device + n_dev // 2, n_dev) - n_dev // 2
    slot_index = (offset_dev + REACH) * patches_here + jnp.mod(listed, patches_here)
    kv_list = [window[offset] for offset in range(-REACH, REACH + 1)]
    n_mp = lax.axis_size("mp")
    kv_spec = pl.BlockSpec((row_count, 2 * width), lambda p, slots: (0, 0))
    partial_value = pl.pallas_call(
        functools.partial(window_attention, n_heads=heads_here, n_win=n_win, n_nb=K_NB),
        grid_spec=pltpu.PrefetchScalarGridSpec(
            num_scalar_prefetch=1,
            grid=(patches_here,),
            in_specs=[pl.BlockSpec((PN, width), lambda p, slots: (p, 0))]
            + [kv_spec] * n_win
            + [pl.BlockSpec((width, D), lambda p, slots: (0, 0))],
            out_specs=pl.BlockSpec((n_mp, PN, D // n_mp), lambda p, slots: (0, p, 0)),
            scratch_shapes=[
                pltpu.VMEM((PN, width), jnp.bfloat16),
                pltpu.VMEM((K_NB * PN, 2 * width), jnp.bfloat16),
            ],
        ),
        out_shape=jax.ShapeDtypeStruct((n_mp, row_count, D // n_mp), jnp.bfloat16),
    )(slot_index.astype(jnp.int32), queries, *kv_list, w_out)
    col_share = scatter_sum(partial_value)
    col_width = col_share.shape[1]
    col_begin = lax.axis_index("mp") * col_width
    residual_cols = (
        lax.dynamic_slice_in_dim(features, col_begin, col_width, 1).astype(jnp.float32) + col_share
    )
    gain_cols = lax.dynamic_slice_in_dim(gain_mlp, col_begin, col_width, 0)
    square_sum = gather_sum(jnp.sum(residual_cols * residual_cols, axis=1), n_mp)
    inverse_rms = lax.rsqrt(square_sum / D + 1e-05)
    normed_cols = (residual_cols * inverse_rms[:, None] * gain_cols).astype(jnp.bfloat16)
    normed2 = gather_cols(normed_cols, n_mp)
    hidden = jax.nn.gelu(
        jnp.dot(normed2, w_up, preferred_element_type=jnp.float32), approximate=True
    ).astype(jnp.bfloat16)
    down_term = jnp.dot(hidden, w_down, preferred_element_type=jnp.float32)
    down_cols = scatter_cols(down_term.astype(jnp.bfloat16), n_mp)
    return (residual_cols + down_cols).astype(jnp.bfloat16)


def solution(mesh):
    return jax.shard_map(
        per_device,
        mesh=mesh,
        in_specs=(
            P("patch", None),
            P(),
            P(None, None, "mp"),
            P("mp", None),
            P(),
            P(None, "mp"),
            P("mp", None),
            P(),
        ),
        out_specs=P("patch", "mp"),
        check_vma=False,
    )
```

```python
import functools

import jax
import jax.numpy as jnp
from jax import lax
from jax.experimental import pallas as pl
from jax.experimental.pallas import tpu as pltpu
from jax.sharding import PartitionSpec as P

D = 1024
HD = 64
PN = 128
K_NB = 8
REACH = 2


def from_behind(array, axis, by):
    length = lax.axis_size(axis)
    return lax.ppermute(array, axis, [(i, (i + by) % length) for i in range(length)])


def normalize(rows, gain):
    rows32 = rows.astype(jnp.float32)
    mean_sq = jnp.mean(rows32 * rows32, axis=-1, keepdims=True)
    return (rows32 * lax.rsqrt(mean_sq + 1e-05) * gain).astype(jnp.bfloat16)


def scatter_sum(parts, n_mp):
    rows, cols = parts.shape
    got = lax.all_to_all(parts.reshape(rows, n_mp, cols // n_mp), "mp", 1, 1)
    total = got[:, 0].astype(jnp.float32)
    for which in range(1, n_mp):
        total = total + got[:, which].astype(jnp.float32)
    return total


def gather_sum(vector, n_mp):
    got = lax.all_to_all(jnp.broadcast_to(vector[None], (n_mp,) + vector.shape), "mp", 0, 0)
    total = got[0]
    for which in range(1, n_mp):
        total = total + got[which]
    return total


def gather_cols(block, n_mp):
    rows, cols = block.shape
    spread = jnp.broadcast_to(block[:, None], (rows, n_mp, cols))
    return lax.all_to_all(spread, "mp", 1, 1).reshape(rows, n_mp * cols)


def window_attention(slot_ref, query_ref, *refs, n_heads, n_win, n_nb):
    kv_refs, out_ref, gathered = refs[:n_win], refs[n_win], refs[n_win + 1]
    width = n_heads * HD
    per_win = kv_refs[0].shape[0] // PN
    lane = lax.broadcasted_iota(jnp.int32, (PN, 2 * HD), 1)
    for patch in range(query_ref.shape[0] // PN):
        rows = slice(patch * PN, (patch + 1) * PN)
        for k in range(n_nb):
            slot = slot_ref[patch, k]
            block = slot // per_win
            local = slot % per_win
            for w in range(n_win):
                @pl.when(block == w)
                def _():
                    start = pl.multiple_of(local * PN, PN)
                    gathered[k * PN:(k + 1) * PN, :] = kv_refs[w][pl.ds(start, PN), :]
        for pair in range(n_heads // 2):
            cols = slice(pair * 2 * HD, (pair + 1) * 2 * HD)
            v_cols = slice(width + pair * 2 * HD, width + (pair + 1) * 2 * HD)
            q_pair = query_ref[rows, cols]
            keys = gathered[:, cols]
            vals = gathered[:, v_cols]
            mixed = []
            for half in range(2):
                keep = (lane >= half * HD) & (lane < (half + 1) * HD)
                q_head = jnp.where(keep, q_pair, jnp.zeros_like(q_pair))
                s = lax.dot_general(
                    q_head, keys, (((1,), (1,)), ((), ())), preferred_element_type=jnp.float32
                ) * (1.0 / HD**0.5)
                e = jnp.exp(s - s.max(axis=1, keepdims=True))
                inv = 1.0 / e.sum(axis=1, keepdims=True)
                probs = (e * inv).astype(jnp.bfloat16)
                mixed.append(jnp.dot(probs, vals, preferred_element_type=jnp.float32))
            out = jnp.where(lane < HD, mixed[0], mixed[1])
            out_ref[rows, cols] = out.astype(out_ref.dtype)


def per_device(features, gain_attn, w_qkv, w_out, gain_mlp, w_up, w_down, neighbours):
    row_count = features.shape[0]
    patches_here = row_count // PN
    width = w_qkv.shape[2]
    heads_here = width // HD
    n_win = 2 * REACH + 1
    normed = normalize(features, gain_attn)
    w_all = jnp.concatenate([w_qkv[0], w_qkv[1], w_qkv[2]], axis=1)
    qkv = jnp.dot(normed, w_all, preferred_element_type=jnp.float32).astype(jnp.bfloat16)
    queries = qkv[:, :width]
    own_kv = qkv[:, width:]
    window = {0: own_kv}
    for offset in range(-REACH, REACH + 1):
        if offset != 0:
            window[offset] = from_behind(own_kv, "patch", -offset)
    device = lax.axis_index("patch")
    n_dev = lax.axis_size("patch")
    listed = lax.dynamic_slice_in_dim(neighbours, device * patches_here, patches_here, 0)
    owner_dev = listed // patches_here
    offset_dev = jnp.mod(owner_dev - device + n_dev // 2, n_dev) - n_dev // 2
    slot_index = (offset_dev + REACH) * patches_here + jnp.mod(listed, patches_here)
    kv_list = [window[offset] for offset in range(-REACH, REACH + 1)]
    kv_spec = pl.BlockSpec((row_count, 2 * width), lambda p, slots: (0, 0))
    attended = pl.pallas_call(
        functools.partial(window_attention, n_heads=heads_here, n_win=n_win, n_nb=K_NB),
        grid_spec=pltpu.PrefetchScalarGridSpec(
            num_scalar_prefetch=1,
            grid=(1,),
            in_specs=[pl.BlockSpec((row_count, width), lambda p, slots: (0, 0))] + [kv_spec] * n_win,
            out_specs=pl.BlockSpec((row_count, width), lambda p, slots: (0, 0)),
            scratch_shapes=[pltpu.VMEM((K_NB * PN, 2 * width), jnp.bfloat16)],
        ),
        out_shape=jax.ShapeDtypeStruct((row_count, width), jnp.bfloat16),
    )(slot_index.astype(jnp.int32), queries, *kv_list)
    n_mp = lax.axis_size("mp")
    partial_value = jnp.dot(attended, w_out, preferred_element_type=jnp.float32)
    col_share = scatter_sum(partial_value.astype(jnp.bfloat16), n_mp)
    col_width = col_share.shape[1]
    col_begin = lax.axis_index("mp") * col_width
    residual_cols = (
        lax.dynamic_slice_in_dim(features, col_begin, col_width, 1).astype(jnp.float32) + col_share
    )
    gain_cols = lax.dynamic_slice_in_dim(gain_mlp, col_begin, col_width, 0)
    square_sum = gather_sum(jnp.sum(residual_cols * residual_cols, axis=1), n_mp)
    inverse_rms = lax.rsqrt(square_sum / D + 1e-05)
    normed_cols = (residual_cols * inverse_rms[:, None] * gain_cols).astype(jnp.bfloat16)
    normed2 = gather_cols(normed_cols, n_mp)
    hidden = jax.nn.gelu(
        jnp.dot(normed2, w_up, preferred_element_type=jnp.float32), approximate=True
    ).astype(jnp.bfloat16)
    down_term = jnp.dot(hidden, w_down, preferred_element_type=jnp.float32)
    down_cols = scatter_sum(down_term.astype(jnp.bfloat16), n_mp)
    return (residual_cols + down_cols).astype(jnp.bfloat16)


def solution(mesh):
    return jax.shard_map(
        per_device,
        mesh=mesh,
        in_specs=(
            P("patch", None),
            P(),
            P(None, None, "mp"),
            P("mp", None),
            P(),
            P(None, "mp"),
            P("mp", None),
            P(),
        ),
        out_specs=P("patch", "mp"),
        check_vma=False,
    )
```

```python
import functools

import jax
import jax.numpy as jnp
from jax import lax
from jax.experimental import pallas as pl
from jax.experimental.pallas import tpu as pltpu
from jax.sharding import PartitionSpec as P

D = 1024
HD = 64
PN = 128
K_NB = 8
REACH = 2


def from_behind(array, axis, by):
    length = lax.axis_size(axis)
    return lax.ppermute(array, axis, [(i, (i + by) % length) for i in range(length)])


def normalize(rows, gain):
    rows32 = rows.astype(jnp.float32)
    mean_sq = jnp.mean(rows32 * rows32, axis=-1, keepdims=True)
    return (rows32 * lax.rsqrt(mean_sq + 1e-05) * gain).astype(jnp.bfloat16)


def scatter_sum(parts, n_mp):
    rows, cols = parts.shape
    got = lax.all_to_all(parts.reshape(rows, n_mp, cols // n_mp), "mp", 1, 1)
    total = got[:, 0].astype(jnp.float32)
    for which in range(1, n_mp):
        total = total + got[:, which].astype(jnp.float32)
    return total


def gather_sum(vector, n_mp):
    got = lax.all_to_all(jnp.broadcast_to(vector[None], (n_mp,) + vector.shape), "mp", 0, 0)
    total = got[0]
    for which in range(1, n_mp):
        total = total + got[which]
    return total


def gather_cols(block, n_mp):
    rows, cols = block.shape
    spread = jnp.broadcast_to(block[:, None], (rows, n_mp, cols))
    return lax.all_to_all(spread, "mp", 1, 1).reshape(rows, n_mp * cols)


def window_attention(slot_ref, query_ref, *refs, n_heads, n_win, n_nb):
    kv_refs, out_ref, gathered = refs[:n_win], refs[n_win], refs[n_win + 1]
    width = n_heads * HD
    per_win = kv_refs[0].shape[0] // PN
    patch = pl.program_id(0)
    for k in range(n_nb):
        slot = slot_ref[patch, k]
        block = slot // per_win
        local = slot % per_win
        for w in range(n_win):
            @pl.when(block == w)
            def _():
                gathered[k * PN:(k + 1) * PN, :] = kv_refs[w][pl.ds(pl.multiple_of(local * PN, PN), PN), :]
    lane = lax.broadcasted_iota(jnp.int32, (PN, 2 * HD), 1)
    for pair in range(n_heads // 2):
        cols = slice(pair * 2 * HD, (pair + 1) * 2 * HD)
        v_cols = slice(width + pair * 2 * HD, width + (pair + 1) * 2 * HD)
        q_pair = query_ref[:, cols]
        keys = gathered[:, cols]
        vals = gathered[:, v_cols]
        mixed = []
        for half in range(2):
            keep = (lane >= half * HD) & (lane < (half + 1) * HD)
            q_head = jnp.where(keep, q_pair, jnp.zeros_like(q_pair))
            s = lax.dot_general(
                q_head, keys, (((1,), (1,)), ((), ())), preferred_element_type=jnp.float32
            ) * (1.0 / HD**0.5)
            e = jnp.exp(s - s.max(axis=1, keepdims=True))
            inv = 1.0 / e.sum(axis=1, keepdims=True)
            probs = (e * inv).astype(jnp.bfloat16)
            mixed.append(jnp.dot(probs, vals, preferred_element_type=jnp.float32))
        out = jnp.where(lane < HD, mixed[0], mixed[1])
        out_ref[:, cols] = out.astype(out_ref.dtype)


def per_device(features, gain_attn, w_qkv, w_out, gain_mlp, w_up, w_down, neighbours):
    row_count = features.shape[0]
    patches_here = row_count // PN
    width = w_qkv.shape[2]
    heads_here = width // HD
    n_win = 2 * REACH + 1
    normed = normalize(features, gain_attn)
    projected = [
        jnp.dot(normed, w_qkv[which], preferred_element_type=jnp.float32).astype(jnp.bfloat16)
        for which in range(3)
    ]
    queries = projected[0]
    own_kv = jnp.concatenate(projected[1:], axis=1)
    window = {0: own_kv}
    for offset in range(-REACH, REACH + 1):
        if offset != 0:
            window[offset] = from_behind(own_kv, "patch", -offset)
    device = lax.axis_index("patch")
    n_dev = lax.axis_size("patch")
    listed = lax.dynamic_slice_in_dim(neighbours, device * patches_here, patches_here, 0)
    owner_dev = listed // patches_here
    offset_dev = jnp.mod(owner_dev - device + n_dev // 2, n_dev) - n_dev // 2
    slot_index = (offset_dev + REACH) * patches_here + jnp.mod(listed, patches_here)
    kv_list = [window[offset] for offset in range(-REACH, REACH + 1)]
    kv_spec = pl.BlockSpec((row_count, 2 * width), lambda p, slots: (0, 0))
    attended = pl.pallas_call(
        functools.partial(window_attention, n_heads=heads_here, n_win=n_win, n_nb=K_NB),
        grid_spec=pltpu.PrefetchScalarGridSpec(
            num_scalar_prefetch=1,
            grid=(patches_here,),
            in_specs=[pl.BlockSpec((PN, width), lambda p, slots: (p, 0))] + [kv_spec] * n_win,
            out_specs=pl.BlockSpec((PN, width), lambda p, slots: (p, 0)),
            scratch_shapes=[pltpu.VMEM((K_NB * PN, 2 * width), jnp.bfloat16)],
        ),
        out_shape=jax.ShapeDtypeStruct((row_count, width), jnp.bfloat16),
    )(slot_index.astype(jnp.int32), queries, *kv_list)
    n_mp = lax.axis_size("mp")
    partial_value = jnp.dot(attended, w_out, preferred_element_type=jnp.float32)
    col_share = scatter_sum(partial_value.astype(jnp.bfloat16), n_mp)
    col_width = col_share.shape[1]
    col_begin = lax.axis_index("mp") * col_width
    residual_cols = (
        lax.dynamic_slice_in_dim(features, col_begin, col_width, 1).astype(jnp.float32) + col_share
    )
    gain_cols = lax.dynamic_slice_in_dim(gain_mlp, col_begin, col_width, 0)
    square_sum = gather_sum(jnp.sum(residual_cols * residual_cols, axis=1), n_mp)
    inverse_rms = lax.rsqrt(square_sum / D + 1e-05)
    normed_cols = (residual_cols * inverse_rms[:, None] * gain_cols).astype(jnp.bfloat16)
    normed2 = gather_cols(normed_cols, n_mp)
    hidden = jax.nn.gelu(
        jnp.dot(normed2, w_up, preferred_element_type=jnp.float32), approximate=True
    ).astype(jnp.bfloat16)
    down_term = jnp.dot(hidden, w_down, preferred_element_type=jnp.float32)
    down_cols = scatter_sum(down_term.astype(jnp.bfloat16), n_mp)
    return (residual_cols + down_cols).astype(jnp.bfloat16)


def solution(mesh):
    return jax.shard_map(
        per_device,
        mesh=mesh,
        in_specs=(
            P("patch", None),
            P(),
            P(None, None, "mp"),
            P("mp", None),
            P(),
            P(None, "mp"),
            P("mp", None),
            P(),
        ),
        out_specs=P("patch", "mp"),
        check_vma=False,
    )
```

```python
import functools

import jax
import jax.numpy as jnp
from jax import lax
from jax.experimental import pallas as pl
from jax.experimental.pallas import tpu as pltpu
from jax.sharding import PartitionSpec as P

D = 1024
HD = 64
PN = 128
K_NB = 8
REACH = 2


def from_behind(array, axis, by):
    length = lax.axis_size(axis)
    return lax.ppermute(array, axis, [(i, (i + by) % length) for i in range(length)])


def normalize(rows, gain):
    rows32 = rows.astype(jnp.float32)
    mean_sq = jnp.mean(rows32 * rows32, axis=-1, keepdims=True)
    return (rows32 * lax.rsqrt(mean_sq + 1e-05) * gain).astype(jnp.bfloat16)


def scatter_sum(parts, n_mp):
    rows, cols = parts.shape
    got = lax.all_to_all(parts.reshape(rows, n_mp, cols // n_mp), "mp", 1, 1)
    total = got[:, 0].astype(jnp.float32)
    for which in range(1, n_mp):
        total = total + got[:, which].astype(jnp.float32)
    return total


def gather_sum(vector, n_mp):
    got = lax.all_to_all(jnp.broadcast_to(vector[None], (n_mp,) + vector.shape), "mp", 0, 0)
    total = got[0]
    for which in range(1, n_mp):
        total = total + got[which]
    return total


def gather_cols(block, n_mp):
    rows, cols = block.shape
    spread = jnp.broadcast_to(block[:, None], (rows, n_mp, cols))
    return lax.all_to_all(spread, "mp", 1, 1).reshape(rows, n_mp * cols)


def project_qkv(x_ref, inv_ref, gain_ref, w_ref, out_ref):
    normed = (x_ref[...].astype(jnp.float32) * inv_ref[...] * gain_ref[...]).astype(jnp.bfloat16)
    out_ref[0] = jnp.dot(normed, w_ref[0], preferred_element_type=jnp.float32).astype(out_ref.dtype)


def window_attention(slot_ref, query_ref, *refs, n_heads, n_win, n_nb):
    kv_refs, out_ref, gathered = refs[:n_win], refs[n_win], refs[n_win + 1]
    per_win = kv_refs[0].shape[1] // PN
    patch = pl.program_id(0)
    for k in range(n_nb):
        slot = slot_ref[patch, k]
        block = slot // per_win
        local = slot % per_win
        for w in range(n_win):
            @pl.when(block == w)
            def _():
                start = pl.multiple_of(local * PN, PN)
                gathered[:, k * PN:(k + 1) * PN, :] = kv_refs[w][:, pl.ds(start, PN), :]
    lane = lax.broadcasted_iota(jnp.int32, (PN, 2 * HD), 1)
    for pair in range(n_heads // 2):
        cols = slice(pair * 2 * HD, (pair + 1) * 2 * HD)
        q_pair = query_ref[:, cols] * jnp.asarray(1.0 / HD**0.5, query_ref.dtype)
        keys = gathered[0, :, cols]
        vals = gathered[1, :, cols]
        mixed = []
        for half in range(2):
            keep = (lane >= half * HD) & (lane < (half + 1) * HD)
            q_head = jnp.where(keep, q_pair, jnp.zeros_like(q_pair))
            s = lax.dot_general(
                q_head, keys, (((1,), (1,)), ((), ())), preferred_element_type=jnp.float32
            )
            e = jnp.exp(s - s.max(axis=1, keepdims=True))
            inv = 1.0 / e.sum(axis=1, keepdims=True)
            probs = (e * inv).astype(jnp.bfloat16)
            mixed.append(jnp.dot(probs, vals, preferred_element_type=jnp.float32))
        out = jnp.where(lane < HD, mixed[0], mixed[1])
        out_ref[:, cols] = out.astype(out_ref.dtype)


def per_device(features, gain_attn, w_qkv, w_out, gain_mlp, w_up, w_down, neighbours):
    row_count = features.shape[0]
    patches_here = row_count // PN
    width = w_qkv.shape[2]
    heads_here = width // HD
    n_win = 2 * REACH + 1
    rows32 = features.astype(jnp.float32)
    inverse = lax.rsqrt(jnp.mean(rows32 * rows32, axis=-1, keepdims=True) + 1e-05)
    qkv = pl.pallas_call(
        project_qkv,
        grid=(3,),
        in_specs=[
            pl.BlockSpec((row_count, D), lambda t: (0, 0)),
            pl.BlockSpec((row_count, 1), lambda t: (0, 0)),
            pl.BlockSpec((1, D), lambda t: (0, 0)),
            pl.BlockSpec((1, D, width), lambda t: (t, 0, 0)),
        ],
        out_specs=pl.BlockSpec((1, row_count, width), lambda t: (t, 0, 0)),
        out_shape=jax.ShapeDtypeStruct((3, row_count, width), jnp.bfloat16),
    )(features, inverse, gain_attn.reshape(1, D), w_qkv)
    queries = qkv[0]
    own_kv = qkv[1:]
    window = {0: own_kv}
    for offset in range(-REACH, REACH + 1):
        if offset != 0:
            window[offset] = from_behind(own_kv, "patch", -offset)
    device = lax.axis_index("patch")
    n_dev = lax.axis_size("patch")
    listed = lax.dynamic_slice_in_dim(neighbours, device * patches_here, patches_here, 0)
    owner_dev = listed // patches_here
    offset_dev = jnp.mod(owner_dev - device + n_dev // 2, n_dev) - n_dev // 2
    slot_index = (offset_dev + REACH) * patches_here + jnp.mod(listed, patches_here)
    kv_list = [window[offset] for offset in range(-REACH, REACH + 1)]
    kv_spec = pl.BlockSpec((2, row_count, width), lambda p, slots: (0, 0, 0))
    attended = pl.pallas_call(
        functools.partial(window_attention, n_heads=heads_here, n_win=n_win, n_nb=K_NB),
        grid_spec=pltpu.PrefetchScalarGridSpec(
            num_scalar_prefetch=1,
            grid=(patches_here,),
            in_specs=[pl.BlockSpec((PN, width), lambda p, slots: (p, 0))] + [kv_spec] * n_win,
            out_specs=pl.BlockSpec((PN, width), lambda p, slots: (p, 0)),
            scratch_shapes=[pltpu.VMEM((2, K_NB * PN, width), jnp.bfloat16)],
        ),
        out_shape=jax.ShapeDtypeStruct((row_count, width), jnp.bfloat16),
    )(slot_index.astype(jnp.int32), queries, *kv_list)
    n_mp = lax.axis_size("mp")
    partial_value = jnp.dot(attended, w_out, preferred_element_type=jnp.float32)
    col_share = scatter_sum(partial_value.astype(jnp.bfloat16), n_mp)
    col_width = col_share.shape[1]
    col_begin = lax.axis_index("mp") * col_width
    residual_cols = (
        lax.dynamic_slice_in_dim(features, col_begin, col_width, 1).astype(jnp.float32) + col_share
    )
    gain_cols = lax.dynamic_slice_in_dim(gain_mlp, col_begin, col_width, 0)
    square_sum = gather_sum(jnp.sum(residual_cols * residual_cols, axis=1), n_mp)
    inverse_rms = lax.rsqrt(square_sum / D + 1e-05)
    normed_cols = (residual_cols * inverse_rms[:, None] * gain_cols).astype(jnp.bfloat16)
    normed2 = gather_cols(normed_cols, n_mp)
    hidden = jax.nn.gelu(
        jnp.dot(normed2, w_up, preferred_element_type=jnp.float32), approximate=True
    ).astype(jnp.bfloat16)
    down_term = jnp.dot(hidden, w_down, preferred_element_type=jnp.float32)
    down_cols = scatter_sum(down_term.astype(jnp.bfloat16), n_mp)
    return (residual_cols + down_cols).astype(jnp.bfloat16)


def solution(mesh):
    return jax.shard_map(
        per_device,
        mesh=mesh,
        in_specs=(
            P("patch", None),
            P(),
            P(None, None, "mp"),
            P("mp", None),
            P(),
            P(None, "mp"),
            P("mp", None),
            P(),
        ),
        out_specs=P("patch", "mp"),
        check_vma=False,
    )
```

```python
import functools

import jax
import jax.numpy as jnp
from jax import lax
from jax.experimental import pallas as pl
from jax.experimental.pallas import tpu as pltpu
from jax.sharding import PartitionSpec as P

D = 1024
HD = 64
PN = 128
K_NB = 8
REACH = 2


def from_behind(array, axis, by):
    length = lax.axis_size(axis)
    return lax.ppermute(array, axis, [(i, (i + by) % length) for i in range(length)])


def normalize(rows, gain):
    rows32 = rows.astype(jnp.float32)
    mean_sq = jnp.mean(rows32 * rows32, axis=-1, keepdims=True)
    return (rows32 * lax.rsqrt(mean_sq + 1e-05) * gain).astype(jnp.bfloat16)


def scatter_sum(parts, n_mp):
    rows, cols = parts.shape
    got = lax.all_to_all(parts.reshape(rows, n_mp, cols // n_mp), "mp", 1, 1)
    total = got[:, 0].astype(jnp.float32)
    for which in range(1, n_mp):
        total = total + got[:, which].astype(jnp.float32)
    return total


def gather_sum(vector, n_mp):
    got = lax.all_to_all(jnp.broadcast_to(vector[None], (n_mp,) + vector.shape), "mp", 0, 0)
    total = got[0]
    for which in range(1, n_mp):
        total = total + got[which]
    return total


def gather_cols(block, n_mp):
    rows, cols = block.shape
    spread = jnp.broadcast_to(block[:, None], (rows, n_mp, cols))
    return lax.all_to_all(spread, "mp", 1, 1).reshape(rows, n_mp * cols)


def window_attention(slot_ref, query_ref, *refs, n_heads, n_win, n_nb):
    kv_refs, out_ref, gathered = refs[:n_win], refs[n_win], refs[n_win + 1]
    width = n_heads * HD
    per_win = kv_refs[0].shape[0] // PN
    patch = pl.program_id(0)
    for k in range(n_nb):
        slot = slot_ref[patch, k]
        block = slot // per_win
        local = slot % per_win
        for w in range(n_win):
            @pl.when(block == w)
            def _():
                gathered[k * PN:(k + 1) * PN, :] = kv_refs[w][pl.ds(pl.multiple_of(local * PN, PN), PN), :]
    lane = lax.broadcasted_iota(jnp.int32, (PN, 2 * HD), 1)
    for pair in range(n_heads // 2):
        cols = slice(pair * 2 * HD, (pair + 1) * 2 * HD)
        v_cols = slice(width + pair * 2 * HD, width + (pair + 1) * 2 * HD)
        q_pair = query_ref[:, cols]
        keys = gathered[:, cols]
        vals = gathered[:, v_cols]
        mixed = []
        for half in range(2):
            keep = (lane >= half * HD) & (lane < (half + 1) * HD)
            q_head = jnp.where(keep, q_pair, jnp.zeros_like(q_pair))
            s = lax.dot_general(
                q_head, keys, (((1,), (1,)), ((), ())), preferred_element_type=jnp.float32
            ) * (1.0 / HD**0.5)
            e = jnp.exp(s - s.max(axis=1, keepdims=True))
            inv = 1.0 / e.sum(axis=1, keepdims=True)
            probs = (e * inv).astype(jnp.bfloat16)
            mixed.append(jnp.dot(probs, vals, preferred_element_type=jnp.float32))
        out = jnp.where(lane < HD, mixed[0], mixed[1])
        out_ref[:, cols] = out.astype(out_ref.dtype)


def per_device(features, gain_attn, w_qkv, w_out, gain_mlp, w_up, w_down, neighbours):
    row_count = features.shape[0]
    patches_here = row_count // PN
    width = w_qkv.shape[2]
    heads_here = width // HD
    n_win = 2 * REACH + 1
    normed = normalize(features, gain_attn)
    qkv = jnp.einsum(
        "rk,tkc->rtc", normed, w_qkv, preferred_element_type=jnp.float32
    ).astype(jnp.bfloat16).reshape(row_count, 3 * width)
    queries = qkv[:, :width]
    own_kv = qkv[:, width:]
    window = {0: own_kv}
    for offset in range(-REACH, REACH + 1):
        if offset != 0:
            window[offset] = from_behind(own_kv, "patch", -offset)
    device = lax.axis_index("patch")
    n_dev = lax.axis_size("patch")
    listed = lax.dynamic_slice_in_dim(neighbours, device * patches_here, patches_here, 0)
    owner_dev = listed // patches_here
    offset_dev = jnp.mod(owner_dev - device + n_dev // 2, n_dev) - n_dev // 2
    slot_index = (offset_dev + REACH) * patches_here + jnp.mod(listed, patches_here)
    kv_list = [window[offset] for offset in range(-REACH, REACH + 1)]
    kv_spec = pl.BlockSpec((row_count, 2 * width), lambda p, slots: (0, 0))
    attended = pl.pallas_call(
        functools.partial(window_attention, n_heads=heads_here, n_win=n_win, n_nb=K_NB),
        grid_spec=pltpu.PrefetchScalarGridSpec(
            num_scalar_prefetch=1,
            grid=(patches_here,),
            in_specs=[pl.BlockSpec((PN, width), lambda p, slots: (p, 0))] + [kv_spec] * n_win,
            out_specs=pl.BlockSpec((PN, width), lambda p, slots: (p, 0)),
            scratch_shapes=[pltpu.VMEM((K_NB * PN, 2 * width), jnp.bfloat16)],
        ),
        out_shape=jax.ShapeDtypeStruct((row_count, width), jnp.bfloat16),
    )(slot_index.astype(jnp.int32), queries, *kv_list)
    n_mp = lax.axis_size("mp")
    partial_value = jnp.dot(attended, w_out, preferred_element_type=jnp.float32)
    col_share = scatter_sum(partial_value.astype(jnp.bfloat16), n_mp)
    col_width = col_share.shape[1]
    col_begin = lax.axis_index("mp") * col_width
    residual_cols = (
        lax.dynamic_slice_in_dim(features, col_begin, col_width, 1).astype(jnp.float32) + col_share
    )
    gain_cols = lax.dynamic_slice_in_dim(gain_mlp, col_begin, col_width, 0)
    square_sum = gather_sum(jnp.sum(residual_cols * residual_cols, axis=1), n_mp)
    inverse_rms = lax.rsqrt(square_sum / D + 1e-05)
    normed_cols = (residual_cols * inverse_rms[:, None] * gain_cols).astype(jnp.bfloat16)
    normed2 = gather_cols(normed_cols, n_mp)
    hidden = jax.nn.gelu(
        jnp.dot(normed2, w_up, preferred_element_type=jnp.float32), approximate=True
    ).astype(jnp.bfloat16)
    down_term = jnp.dot(hidden, w_down, preferred_element_type=jnp.float32)
    down_cols = scatter_sum(down_term.astype(jnp.bfloat16), n_mp)
    return (residual_cols + down_cols).astype(jnp.bfloat16)


def solution(mesh):
    return jax.shard_map(
        per_device,
        mesh=mesh,
        in_specs=(
            P("patch", None),
            P(),
            P(None, None, "mp"),
            P("mp", None),
            P(),
            P(None, "mp"),
            P("mp", None),
            P(),
        ),
        out_specs=P("patch", "mp"),
        check_vma=False,
    )
```

```python
import functools

import jax
import jax.numpy as jnp
from jax import lax
from jax.experimental import pallas as pl
from jax.experimental.pallas import tpu as pltpu
from jax.sharding import PartitionSpec as P

D = 1024
HD = 64
PN = 128
K_NB = 8
REACH = 2


def from_behind(array, axis, by):
    length = lax.axis_size(axis)
    return lax.ppermute(array, axis, [(i, (i + by) % length) for i in range(length)])


def normalize(rows, gain):
    rows32 = rows.astype(jnp.float32)
    mean_sq = jnp.mean(rows32 * rows32, axis=-1, keepdims=True)
    return (rows32 * lax.rsqrt(mean_sq + 1e-05) * gain).astype(jnp.bfloat16)


def scatter_sum(parts, n_mp):
    rows, cols = parts.shape
    got = lax.all_to_all(parts.reshape(rows, n_mp, cols // n_mp), "mp", 1, 1)
    total = got[:, 0].astype(jnp.float32)
    for which in range(1, n_mp):
        total = total + got[:, which].astype(jnp.float32)
    return total


def gather_sum(vector, n_mp):
    got = lax.all_to_all(jnp.broadcast_to(vector[None], (n_mp,) + vector.shape), "mp", 0, 0)
    total = got[0]
    for which in range(1, n_mp):
        total = total + got[which]
    return total


def gather_cols(block, n_mp):
    rows, cols = block.shape
    spread = jnp.broadcast_to(block[:, None], (rows, n_mp, cols))
    return lax.all_to_all(spread, "mp", 1, 1).reshape(rows, n_mp * cols)


def window_attention(slot_ref, query_ref, *refs, n_heads, n_win, n_nb):
    kv_refs, out_ref, gathered = refs[:n_win], refs[n_win], refs[n_win + 1]
    width = n_heads * HD
    per_win = kv_refs[0].shape[0] // PN
    patch = pl.program_id(0)
    for k in range(n_nb):
        slot = slot_ref[patch, k]
        block = slot // per_win
        local = slot % per_win
        for w in range(n_win):
            @pl.when(block == w)
            def _():
                gathered[k * PN:(k + 1) * PN, :] = kv_refs[w][pl.ds(pl.multiple_of(local * PN, PN), PN), :]
    lane = lax.broadcasted_iota(jnp.int32, (PN, 2 * HD), 1)
    for pair in range(n_heads // 2):
        cols = slice(pair * 2 * HD, (pair + 1) * 2 * HD)
        v_cols = slice(width + pair * 2 * HD, width + (pair + 1) * 2 * HD)
        q_pair = query_ref[:, cols] * jnp.asarray(1.0 / HD**0.5, query_ref.dtype)
        keys = gathered[:, cols]
        vals = gathered[:, v_cols]
        mixed = []
        for half in range(2):
            keep = (lane >= half * HD) & (lane < (half + 1) * HD)
            q_head = jnp.where(keep, q_pair, jnp.zeros_like(q_pair))
            s = lax.dot_general(
                q_head, keys, (((1,), (1,)), ((), ())), preferred_element_type=jnp.float32
            )
            e = jnp.exp(s - s.max(axis=1, keepdims=True))
            inv = 1.0 / e.sum(axis=1, keepdims=True)
            probs = (e * inv).astype(jnp.bfloat16)
            mixed.append(jnp.dot(probs, vals, preferred_element_type=jnp.float32))
        out = jnp.where(lane < HD, mixed[0], mixed[1])
        out_ref[:, cols] = out.astype(out_ref.dtype)


def per_device(features, gain_attn, w_qkv, w_out, gain_mlp, w_up, w_down, neighbours):
    row_count = features.shape[0]
    patches_here = row_count // PN
    width = w_qkv.shape[2]
    heads_here = width // HD
    n_win = 2 * REACH + 1
    normed = normalize(features, gain_attn)
    w_all = jnp.concatenate([w_qkv[0], w_qkv[1], w_qkv[2]], axis=1)
    qkv = jnp.dot(normed, w_all, preferred_element_type=jnp.float32).astype(jnp.bfloat16)
    queries = qkv[:, :width]
    own_kv = qkv[:, width:]
    window = {0: own_kv}
    for offset in range(-REACH, REACH + 1):
        if offset != 0:
            window[offset] = from_behind(own_kv, "patch", -offset)
    device = lax.axis_index("patch")
    n_dev = lax.axis_size("patch")
    listed = lax.dynamic_slice_in_dim(neighbours, device * patches_here, patches_here, 0)
    owner_dev = listed // patches_here
    offset_dev = jnp.mod(owner_dev - device + n_dev // 2, n_dev) - n_dev // 2
    slot_index = (offset_dev + REACH) * patches_here + jnp.mod(listed, patches_here)
    kv_list = [window[offset] for offset in range(-REACH, REACH + 1)]
    kv_spec = pl.BlockSpec((row_count, 2 * width), lambda p, slots: (0, 0))
    attended = pl.pallas_call(
        functools.partial(window_attention, n_heads=heads_here, n_win=n_win, n_nb=K_NB),
        grid_spec=pltpu.PrefetchScalarGridSpec(
            num_scalar_prefetch=1,
            grid=(patches_here,),
            in_specs=[pl.BlockSpec((PN, width), lambda p, slots: (p, 0))] + [kv_spec] * n_win,
            out_specs=pl.BlockSpec((PN, width), lambda p, slots: (p, 0)),
            scratch_shapes=[pltpu.VMEM((K_NB * PN, 2 * width), jnp.bfloat16)],
        ),
        out_shape=jax.ShapeDtypeStruct((row_count, width), jnp.bfloat16),
    )(slot_index.astype(jnp.int32), queries, *kv_list)
    n_mp = lax.axis_size("mp")
    partial_value = jnp.dot(attended, w_out, preferred_element_type=jnp.float32)
    col_share = scatter_sum(partial_value.astype(jnp.bfloat16), n_mp)
    col_width = col_share.shape[1]
    col_begin = lax.axis_index("mp") * col_width
    residual_cols = (
        lax.dynamic_slice_in_dim(features, col_begin, col_width, 1).astype(jnp.float32) + col_share
    )
    gain_cols = lax.dynamic_slice_in_dim(gain_mlp, col_begin, col_width, 0)
    square_sum = gather_sum(jnp.sum(residual_cols * residual_cols, axis=1), n_mp)
    inverse_rms = lax.rsqrt(square_sum / D + 1e-05)
    normed_cols = (residual_cols * inverse_rms[:, None] * gain_cols).astype(jnp.bfloat16)
    normed2 = gather_cols(normed_cols, n_mp)
    hidden = jax.nn.gelu(
        jnp.dot(normed2, w_up, preferred_element_type=jnp.float32), approximate=True
    ).astype(jnp.bfloat16)
    down_term = jnp.dot(hidden, w_down, preferred_element_type=jnp.float32)
    down_cols = scatter_sum(down_term.astype(jnp.bfloat16), n_mp)
    return (residual_cols + down_cols).astype(jnp.bfloat16)


def solution(mesh):
    return jax.shard_map(
        per_device,
        mesh=mesh,
        in_specs=(
            P("patch", None),
            P(),
            P(None, None, "mp"),
            P("mp", None),
            P(),
            P(None, "mp"),
            P("mp", None),
            P(),
        ),
        out_specs=P("patch", "mp"),
        check_vma=False,
    )
```
